256 devices in a mesh: fine: 8 (over x, core), coarse: 32 (over z, y).
Axes of the slice: x: 4, y: 4, z: 8, core: 2. Of those that a mesh axis runs over, the one named last changes fastest.
Arguments:
- query_rows: bfloat16 [65536, 768], P(('coarse', 'fine')), may hold values from -6 to 6
- key_rows: bfloat16 [65536, 768], P(('coarse', 'fine')), may hold values from -6 to 6
- value_rows: bfloat16 [65536, 768], P(('coarse', 'fine')), may hold values from -6 to 6
- distance_slope: float32 [12], replicated, may hold values from 0.4 to 1.6
- out_weight: bfloat16 [768, 768], P('coarse'), may hold values from -0.21875 to 0.21875
Outputs:
- mixed: bfloat16 [65536, 768], P(('coarse', 'fine'))
The draws below stay inside these ranges and needn't reach their ends.
All inputs are finite; a program needn't handle non-finite values.
Results may differ from the reference program's by a relative error of at most 0.0065.
Values may be sent and summed in bfloat16 or wider, within the bound.
No kernel may reach another device: no remote copies, remote signals or barrier semaphores. Data moves between devices by JAX's collectives and lax.ppermute only.
A program may use at most 64 MiB of HBM per device.

```python
import math
import jax
import jax.numpy as jnp
from jax import lax

HEADS = 12
D = 768
BLOCK = 128
TOKENS = 65536


def slow_part(key_phase):
    position = jnp.arange(TOKENS, dtype=jnp.int32)
    phases = jax.random.uniform(key_phase, (12, D), minval=-math.pi, maxval=math.pi)
    total = jnp.zeros((TOKENS, D), jnp.float32)
    for octave in range(1, 13):
        period_len = max(TOKENS // 2 ** octave, 2)
        amplitude = 0.8 if octave <= 6 else 0.35
        angle = (position % period_len).astype(jnp.float32) * (2.0 * math.pi / period_len)
        total = total + amplitude * jnp.sin(angle[:, None] + phases[octave - 1][None, :])
    return total


def paired_draw(key_base):
    seed_key = jax.random.fold_in(key_base, 17)
    key_query = jax.random.fold_in(seed_key, 0)
    key_keyed = jax.random.fold_in(seed_key, 1)
    key_qslow = jax.random.fold_in(seed_key, 4)
    key_kslow = jax.random.fold_in(seed_key, 5)
    shape_all = (TOKENS, D)
    query_slow = slow_part(key_qslow)
    key_slow = slow_part(key_kslow)
    query_draw = jnp.clip(0.8 * jax.random.normal(key_query, shape_all) + query_slow, -6.0, 6.0)
    key_draw = jnp.clip(0.8 * jax.random.normal(key_keyed, shape_all) + key_slow, -6.0, 6.0)
    return (query_draw, key_draw)


def draw_query_rows(key, part):
    return paired_draw(key)[0].astype(jnp.bfloat16)


def draw_key_rows(key, part):
    return paired_draw(key)[1].astype(jnp.bfloat16)


def draw_value_rows(key, part):
    seed_key = jax.random.fold_in(key, 29)
    key_rough, key_phase = jax.random.split(seed_key, 2)
    position = jnp.arange(TOKENS, dtype=jnp.float32)[:, None]
    phases = jax.random.uniform(key_phase, (8, D), minval=-math.pi, maxval=math.pi)
    smooth = jnp.zeros((TOKENS, D), jnp.float32)
    for octave in range(8):
        period_len = TOKENS / 2.0 ** octave
        smooth = smooth + 0.35 * jnp.sin(position * (2.0 * math.pi / period_len) + phases[octave][None, :])
    value_draw = 0.8 * jax.random.normal(key_rough, (TOKENS, D)) + smooth
    return jnp.clip(value_draw, -6.0, 6.0).astype(jnp.bfloat16)


def block_levels(own_key, extent, cuts, least, largest):
    loudness, own = 1.0, jax.random.fold_in(own_key, 6)
    for axis_at, shards_of in cuts:
        heights = jnp.exp(jax.random.uniform(jax.random.fold_in(own, axis_at), (shards_of,), jnp.float32, least / len(cuts), largest / len(cuts)))
        loudness = loudness * jnp.repeat(heights, extent[axis_at] // shards_of).reshape([-1 if axis == axis_at else 1 for axis in range(len(extent))])
    return loudness


def bell_draw(rng, shape, spread, reach, cuts=(), kind=jnp.bfloat16):
    gain = block_levels(rng, shape, cuts, -0.22, 0.18) if cuts else 1.0
    result = jax.random.normal(rng, shape, jnp.float32) * spread * gain
    return jnp.minimum(jnp.maximum(result, -reach), reach).astype(kind)


def setup_inputs(seed: int = 0) -> dict:
    key_list = jax.random.split(jax.random.key(seed), 6)
    query_rows = draw_query_rows(jax.random.fold_in(key_list[5], 71), 0)
    key_rows = draw_key_rows(jax.random.fold_in(key_list[5], 71), 0)
    value_rows = draw_value_rows(jax.random.fold_in(key_list[5], 71), 0)
    distance_slope = jnp.clip(jnp.exp(jax.random.uniform(key_list[3], (HEADS,), jnp.float32, math.log(0.4), math.log(1.6))), 0.4, 1.6)
    out_weight = bell_draw(key_list[4], (D, D), D ** -0.5, 0.21875, ((0, 32),))
    return dict(query_rows=query_rows, key_rows=key_rows, value_rows=value_rows, distance_slope=distance_slope, out_weight=out_weight)


LOG_TWO = math.log(2.0)

def coarsen(row_data):
    dims_all = row_data.shape
    paired = row_data.reshape(dims_all[:-2] + (dims_all[-2] // 2, 2, dims_all[-1])).astype(jnp.float32)
    return ((paired[..., 0, :] + paired[..., 1, :]) * 0.5).astype(jnp.bfloat16)

def attend(queries, key_group, value_group, level_gain):
    groups, query_count, width_all = queries.shape
    key_count = key_group.shape[1]
    head_count = level_gain.shape[0]
    head_size = width_all // head_count
    q_heads = queries.astype(jnp.float32).reshape(groups, query_count, head_count, head_size)
    k_heads = key_group.astype(jnp.float32).reshape(groups, key_count, head_count, head_size)
    v_heads = value_group.astype(jnp.float32).reshape(groups, key_count, head_count, head_size)
    scores = jnp.einsum('gqhe,gkhe->ghqk', q_heads, k_heads) * (1.0 / math.sqrt(head_size)) + level_gain[None, :, None, None]
    row_max = lax.optimization_barrier(jnp.max(scores, axis=3))
    p_weights = jnp.exp(scores - row_max[..., None]).astype(jnp.bfloat16)
    row_sum = lax.optimization_barrier(jnp.sum(p_weights.astype(jnp.float32), axis=3))
    weighted = jnp.einsum('ghqk,gkhe->gqhe', p_weights.astype(jnp.float32), v_heads)
    return (jnp.transpose(row_max, (0, 2, 1)).reshape(groups * query_count, head_count), weighted.reshape(groups * query_count, width_all), jnp.transpose(row_sum, (0, 2, 1)).reshape(groups * query_count, head_count))

def level_stats(q_now, k_now, v_now, level_now, distance_slope):
    row_count, width_all = q_now.shape
    level_gain = level_now * LOG_TWO * (1.0 - distance_slope)
    if level_now == 0:
        pair_len = 2 * BLOCK
        q_grp = q_now.reshape(row_count // pair_len, pair_len, width_all)
        k_grp = k_now.reshape(row_count // pair_len, pair_len, width_all)
        v_grp = v_now.reshape(row_count // pair_len, pair_len, width_all)
    else:
        q_grp = q_now.reshape(row_count // BLOCK, BLOCK, width_all)
        k_grp = k_now.reshape(row_count // (2 * BLOCK), 2, BLOCK, width_all)[:, ::-1].reshape(row_count // BLOCK, BLOCK, width_all)
        v_grp = v_now.reshape(row_count // (2 * BLOCK), 2, BLOCK, width_all)[:, ::-1].reshape(row_count // BLOCK, BLOCK, width_all)
    group_count = q_grp.shape[0]
    batch_len = min(group_count, 16)

    def run_batch(batch_args):
        return attend(batch_args[0], batch_args[1], batch_args[2], level_gain)
    shaped = tuple((member.reshape((group_count // batch_len, batch_len) + member.shape[1:]) for member in (q_grp, k_grp, v_grp)))
    row_max, numer, denom = lax.map(run_batch, shaped)
    head_count = distance_slope.shape[0]
    return (row_max.reshape(row_count, head_count), numer.reshape(row_count, width_all), denom.reshape(row_count, head_count))

def widen(level_stat, factor):
    return tuple((jnp.repeat(member, factor, axis=0) for member in level_stat))

def merge(earlier, latest):
    max_a, numer_a, denom_a = earlier
    max_b, numer_b, denom_b = latest
    row_max = jnp.maximum(max_a, max_b)
    scale_a = jnp.exp(max_a - row_max)
    scale_b = jnp.exp(max_b - row_max)
    row_count, width_all = numer_a.shape
    head_count = row_max.shape[1]
    numer = (numer_a.reshape(row_count, head_count, -1) * scale_a[:, :, None] + numer_b.reshape(row_count, head_count, -1) * scale_b[:, :, None]).reshape(row_count, width_all)
    denom = denom_a * scale_a + denom_b * scale_b
    return (row_max, numer, denom)

def reference(query_rows, key_rows, value_rows, distance_slope, out_weight):
    level_total = (TOKENS // BLOCK).bit_length() - 1
    q_now, k_now, v_now = (query_rows, key_rows, value_rows)
    combined = level_stats(q_now, k_now, v_now, 0, distance_slope)
    for level_now in range(1, level_total):
        q_now, k_now, v_now = (coarsen(q_now), coarsen(k_now), coarsen(v_now))
        far_stat = level_stats(q_now, k_now, v_now, level_now, distance_slope)
        combined = merge(combined, widen(far_stat, 2 ** level_now))
    row_max, numer, denom = combined
    row_count, width_all = numer.shape
    head_count = row_max.shape[1]
    attended = (numer.reshape(row_count, head_count, -1) / denom[:, :, None]).reshape(row_count, width_all).astype(jnp.bfloat16)
    return jnp.dot(attended, out_weight, preferred_element_type=jnp.float32).astype(jnp.bfloat16)
```

```python
import math

import jax
import jax.numpy as jnp
import numpy as np
from jax import lax
from jax.sharding import PartitionSpec as P

BLOCK = 128


LOG_TWO = math.log(2.0)


def coarsen(row_data):
    dims_all = row_data.shape
    paired = row_data.reshape(dims_all[:-2] + (dims_all[-2] // 2, 2, dims_all[-1])).astype(
        jnp.float32
    )
    return ((paired[..., 0, :] + paired[..., 1, :]) * 0.5).astype(jnp.bfloat16)


def head_mask(head_count, width_all):
    lane_head = np.arange(width_all) // (width_all // head_count)
    return (lane_head[None, :] == np.arange(head_count)[:, None]).astype(np.float32)


def attend(queries, keys, values, gain):
    batch, query_count, width_all = queries.shape
    key_count = keys.shape[1]
    head_count = gain.shape[-1]
    head_size = width_all // head_count
    lanes = jnp.asarray(head_mask(head_count, width_all), jnp.bfloat16)
    k_spread = (keys[:, None, :, :] * lanes[None, :, None, :]).reshape(
        batch, head_count * key_count, width_all
    )
    v_spread = (values[:, None, :, :] * lanes[None, :, None, :]).reshape(
        batch, head_count * key_count, width_all
    )
    scores = jnp.einsum("bnd,bkd->bnk", queries, k_spread, preferred_element_type=jnp.float32)
    scores = scores.reshape(batch, query_count, head_count, key_count) * (
        1.0 / math.sqrt(head_size)
    ) + gain[:, :, :, None]
    row_max = jnp.max(scores, axis=3)
    p_weights = jnp.exp(scores - row_max[..., None]).astype(jnp.bfloat16)
    row_sum = jnp.sum(p_weights.astype(jnp.float32), axis=3)
    weighted = jnp.einsum(
        "bnk,bkd->bnd",
        p_weights.reshape(batch, query_count, head_count * key_count),
        v_spread,
        preferred_element_type=jnp.float32,
    )
    return row_max, weighted, row_sum


def xor_pairs(size, bit):
    return [(i, i ^ bit) for i in range(size)]


def on_device(query_rows, key_rows, value_rows, distance_slope, out_weight):
    tokens, width_all = query_rows.shape
    head_count = distance_slope.shape[0]
    head_size = width_all // head_count
    fine_size = lax.axis_size("fine")
    coarse_size = lax.axis_size("coarse")
    local_levels = (tokens // BLOCK).bit_length() - 1
    fine_bits = fine_size.bit_length() - 1
    coarse_bits = coarse_size.bit_length() - 1
    level_total = local_levels + fine_bits + coarse_bits
    first_fine = local_levels
    first_coarse = local_levels + fine_bits
    slope_term = LOG_TWO * (1.0 - distance_slope)

    full_weight = lax.all_gather(out_weight, "coarse", axis=0, tiled=True)

    pyramid = [jnp.concatenate([query_rows, key_rows, value_rows], axis=1)]
    for _ in range(1, level_total):
        pyramid.append(coarsen(pyramid[-1]))

    def kv_of(level):
        return pyramid[level][:, width_all:]

    column = {m: kv_of(m) for m in range(first_coarse, level_total)}
    sibling_cols = []
    for bit_no in range(coarse_bits):
        level_now = first_coarse + bit_no
        pending = list(range(level_now, level_total))
        sizes = [column[m].shape[0] for m in pending]
        message = jnp.concatenate([column[m] for m in pending], axis=0)
        received = lax.ppermute(message, "coarse", xor_pairs(coarse_size, 1 << bit_no))
        offsets = np.cumsum([0] + sizes)
        for i, m in enumerate(pending):
            got = received[offsets[i]:offsets[i + 1]]
            if m == level_now:
                sibling_cols.append(got)
            else:
                column[m] = jnp.concatenate([column[m], got], axis=0)

    fine_keys = {l: [] for l in range(first_fine, first_coarse)}
    for offset in range(1, fine_size):
        level_now = first_fine + offset.bit_length() - 1
        fine_keys[level_now].append(
            lax.ppermute(kv_of(level_now), "fine", xor_pairs(fine_size, offset))
        )

    coarse_msg = jnp.concatenate(sibling_cols, axis=0)
    fine_msgs = [coarse_msg]
    for offset in range(1, fine_size):
        fine_msgs.append(lax.ppermute(coarse_msg, "fine", xor_pairs(fine_size, offset)))
    col_rows = sibling_cols[0].shape[0]
    coarse_kv = jnp.stack(fine_msgs).reshape(fine_size, coarse_bits, col_rows, 2 * width_all)
    coarse_kv = jnp.transpose(coarse_kv, (1, 0, 2, 3)).reshape(coarse_bits, -1, 2 * width_all)

    far_kv = jnp.concatenate(
        [jnp.concatenate(fine_keys[l], axis=0)[None] for l in range(first_fine, first_coarse)]
        + [coarse_kv],
        axis=0,
    )
    far_levels = list(range(first_fine, level_total))
    far_q = jnp.stack(
        [
            jnp.pad(pyramid[l][:, :width_all], ((0, BLOCK - pyramid[l].shape[0]), (0, 0)))
            for l in far_levels
        ]
    )
    far_gain = jnp.stack([l * slope_term for l in far_levels])[:, None, :]

    m0, n0, d0 = attend(
        query_rows[None],
        key_rows[None],
        value_rows[None],
        jnp.zeros((1, 1, head_count), jnp.float32),
    )
    mf, nf, df = attend(far_q, far_kv[:, :, :width_all], far_kv[:, :, width_all:], far_gain)

    def widen(x, level):
        return jnp.repeat(x, 1 << level, axis=0)

    def lanes(x):
        return jnp.repeat(x, head_size, axis=1)

    stats = [(0, m0[0], n0[0], d0[0])]
    for i, l in enumerate(far_levels):
        n = tokens >> l
        stats.append((l, mf[i, :n], nf[i, :n], df[i, :n]))
    maxes = [widen(mx, l) for l, mx, _, _ in stats]
    top = maxes[0]
    for mw in maxes[1:]:
        top = jnp.maximum(top, mw)
    numer = None
    denom = None
    for (l, _, nm, dn), mw in zip(stats, maxes):
        scale = jnp.exp(mw - top)
        term_n = widen(nm, l) * lanes(scale)
        term_d = widen(dn, l) * scale
        numer = term_n if numer is None else numer + term_n
        denom = term_d if denom is None else denom + term_d
    attended = (numer / lanes(denom)).astype(jnp.bfloat16)
    projected = jnp.dot(attended, full_weight, preferred_element_type=jnp.float32)
    return projected.astype(jnp.bfloat16)


def solution(mesh):
    return jax.shard_map(
        on_device,
        mesh=mesh,
        in_specs=(
            P(("coarse", "fine"), None),
            P(("coarse", "fine"), None),
            P(("coarse", "fine"), None),
            P(),
            P("coarse", None),
        ),
        out_specs=P(("coarse", "fine"), None),
        check_vma=False,
    )
```

```python
import math

import jax
import jax.numpy as jnp
import numpy as np
from jax import lax
from jax.experimental import pallas as pl
from jax.experimental.pallas import tpu as pltpu
from jax.sharding import PartitionSpec as P

BLOCK = 128


LOG_TWO = math.log(2.0)


def coarsen(row_data):
    dims_all = row_data.shape
    paired = row_data.reshape(dims_all[:-2] + (dims_all[-2] // 2, 2, dims_all[-1])).astype(
        jnp.float32
    )
    return ((paired[..., 0, :] + paired[..., 1, :]) * 0.5).astype(jnp.bfloat16)


def attention_kernel(q0_ref, k0_ref, v0_ref, fq_ref, fkv_ref, gain_ref, w_ref, out_ref, qw_ref, acc_ref):
    tokens, width_all = q0_ref.shape
    far_count = fq_ref.shape[0]
    head_size = 64
    lane_block = 128
    heads_per_block = lane_block // head_size
    head_count = width_all // head_size
    scale = 1.0 / math.sqrt(head_size)
    rows = lax.broadcasted_iota(jnp.int32, (tokens, BLOCK), 0)
    cols = lax.broadcasted_iota(jnp.int32, (tokens, BLOCK), 1)
    for i in range(far_count):
        spread = ((rows >> (i + 1)) == cols).astype(jnp.bfloat16)
        qw_ref[i] = jnp.dot(spread, fq_ref[i], preferred_element_type=jnp.float32).astype(
            jnp.bfloat16
        )
    lane = lax.broadcasted_iota(jnp.int32, (1, lane_block), 1)
    low_half = lane < head_size

    def block_body(j, carry):
        off = pl.multiple_of(j * lane_block, lane_block)
        states = [None] * heads_per_block
        for level in range(far_count + 1):
            if level == 0:
                q = q0_ref[:, pl.ds(off, lane_block)]
                k = k0_ref[:, pl.ds(off, lane_block)]
                v = v0_ref[:, pl.ds(off, lane_block)]
            else:
                q = qw_ref[level - 1, :, pl.ds(off, lane_block)]
                k = fkv_ref[level - 1, :, pl.ds(off, lane_block)]
                v = fkv_ref[level - 1, :, pl.ds(off + width_all, lane_block)]
            for par in range(heads_per_block):
                keep = low_half if par == 0 else jnp.logical_not(low_half)
                qm = jnp.where(keep, q, jnp.zeros_like(q))
                s = lax.dot_general(
                    qm, k, (((1,), (1,)), ((), ())), preferred_element_type=jnp.float32
                )
                s = s * scale + gain_ref[level * head_count + j * heads_per_block + par]
                m = jnp.max(s, axis=1, keepdims=True)
                p = jnp.exp(s - m).astype(jnp.bfloat16)
                d = jnp.sum(p.astype(jnp.float32), axis=1, keepdims=True)
                n = jnp.dot(p, v, preferred_element_type=jnp.float32)
                if states[par] is None:
                    states[par] = (m, n, d)
                else:
                    ma, na, da = states[par]
                    mx = jnp.maximum(ma, m)
                    sa = jnp.exp(ma - mx)
                    sb = jnp.exp(m - mx)
                    states[par] = (mx, na * sa + n * sb, da * sa + d * sb)
        out_lo = states[0][1] / states[0][2]
        out_hi = states[1][1] / states[1][2]
        acc_ref[:, pl.ds(off, lane_block)] = jnp.where(low_half, out_lo, out_hi).astype(
            jnp.bfloat16
        )
        return carry

    lax.fori_loop(0, width_all // lane_block, block_body, 0)
    out_ref[...] = jnp.dot(acc_ref[...], w_ref[...], preferred_element_type=jnp.float32).astype(
        out_ref.dtype
    )


def fused_attention(q0, k0, v0, far_q, far_kv, level_gain, weight):
    tokens, width_all = q0.shape
    vmem = pl.BlockSpec(memory_space=pltpu.VMEM)
    smem = pl.BlockSpec(memory_space=pltpu.SMEM)
    return pl.pallas_call(
        attention_kernel,
        out_shape=jax.ShapeDtypeStruct((tokens, width_all), jnp.bfloat16),
        in_specs=[vmem, vmem, vmem, vmem, vmem, smem, vmem],
        out_specs=vmem,
        scratch_shapes=[
            pltpu.VMEM((far_q.shape[0], tokens, width_all), jnp.bfloat16),
            pltpu.VMEM((tokens, width_all), jnp.bfloat16),
        ],
    )(q0, k0, v0, far_q, far_kv, level_gain, weight)


def xor_pairs(size, bit):
    return [(i, i ^ bit) for i in range(size)]


def on_device(query_rows, key_rows, value_rows, distance_slope, out_weight):
    tokens, width_all = query_rows.shape
    head_count = distance_slope.shape[0]
    head_size = width_all // head_count
    fine_size = lax.axis_size("fine")
    coarse_size = lax.axis_size("coarse")
    local_levels = (tokens // BLOCK).bit_length() - 1
    fine_bits = fine_size.bit_length() - 1
    coarse_bits = coarse_size.bit_length() - 1
    level_total = local_levels + fine_bits + coarse_bits
    first_fine = local_levels
    first_coarse = local_levels + fine_bits
    slope_term = LOG_TWO * (1.0 - distance_slope)

    full_weight = lax.all_gather(out_weight, "coarse", axis=0, tiled=True)

    pyramid = [jnp.concatenate([query_rows, key_rows, value_rows], axis=1)]
    for _ in range(1, level_total):
        pyramid.append(coarsen(pyramid[-1]))

    def kv_of(level):
        return pyramid[level][:, width_all:]

    column = {m: kv_of(m) for m in range(first_coarse, level_total)}
    sibling_cols = []
    for bit_no in range(coarse_bits):
        level_now = first_coarse + bit_no
        pending = list(range(level_now, level_total))
        sizes = [column[m].shape[0] for m in pending]
        message = jnp.concatenate([column[m] for m in pending], axis=0)
        received = lax.ppermute(message, "coarse", xor_pairs(coarse_size, 1 << bit_no))
        offsets = np.cumsum([0] + sizes)
        for i, m in enumerate(pending):
            got = received[offsets[i]:offsets[i + 1]]
            if m == level_now:
                sibling_cols.append(got)
            else:
                column[m] = jnp.concatenate([column[m], got], axis=0)

    fine_keys = {l: [] for l in range(first_fine, first_coarse)}
    for offset in range(1, fine_size):
        level_now = first_fine + offset.bit_length() - 1
        fine_keys[level_now].append(
            lax.ppermute(kv_of(level_now), "fine", xor_pairs(fine_size, offset))
        )

    coarse_msg = jnp.concatenate(sibling_cols, axis=0)
    fine_msgs = [coarse_msg]
    for offset in range(1, fine_size):
        fine_msgs.append(lax.ppermute(coarse_msg, "fine", xor_pairs(fine_size, offset)))
    col_rows = sibling_cols[0].shape[0]
    coarse_kv = jnp.stack(fine_msgs).reshape(fine_size, coarse_bits, col_rows, 2 * width_all)
    coarse_kv = jnp.transpose(coarse_kv, (1, 0, 2, 3)).reshape(coarse_bits, -1, 2 * width_all)

    far_kv = jnp.concatenate(
        [jnp.concatenate(fine_keys[l], axis=0)[None] for l in range(first_fine, first_coarse)]
        + [coarse_kv],
        axis=0,
    )
    far_levels = list(range(first_fine, level_total))
    far_q = jnp.stack(
        [
            jnp.pad(pyramid[l][:, :width_all], ((0, BLOCK - pyramid[l].shape[0]), (0, 0)))
            for l in far_levels
        ]
    )

    level_gain = jnp.concatenate([l * slope_term for l in range(level_total)])
    return fused_attention(
        query_rows, key_rows, value_rows, far_q, far_kv, level_gain, full_weight
    )


def solution(mesh):
    return jax.shard_map(
        on_device,
        mesh=mesh,
        in_specs=(
            P(("coarse", "fine"), None),
            P(("coarse", "fine"), None),
            P(("coarse", "fine"), None),
            P(),
            P("coarse", None),
        ),
        out_specs=P(("coarse", "fine"), None),
        check_vma=False,
    )
```

```python
import functools
import math

import jax
import jax.numpy as jnp
import numpy as np
from jax import lax
from jax.experimental import pallas as pl
from jax.experimental.pallas import tpu as pltpu
from jax.sharding import PartitionSpec as P

BLOCK = 128


LOG_TWO = math.log(2.0)


def coarsen(row_data):
    dims_all = row_data.shape
    paired = row_data.reshape(dims_all[:-2] + (dims_all[-2] // 2, 2, dims_all[-1])).astype(
        jnp.float32
    )
    return ((paired[..., 0, :] + paired[..., 1, :]) * 0.5).astype(jnp.bfloat16)


HEAD_SIZE = 64
LANE_BLOCK = 128


def widen_queries(fq_ref, qw_ref, first_level):
    tokens = qw_ref.shape[1]
    rows = lax.broadcasted_iota(jnp.int32, (tokens, BLOCK), 0)
    cols = lax.broadcasted_iota(jnp.int32, (tokens, BLOCK), 1)
    for i in range(fq_ref.shape[0]):
        spread = ((rows >> (first_level + i)) == cols).astype(jnp.bfloat16)
        qw_ref[i] = jnp.dot(spread, fq_ref[i], preferred_element_type=jnp.float32).astype(
            jnp.bfloat16
        )


def level_step(states, q, k, v, gains, low_half):
    scale = 1.0 / math.sqrt(HEAD_SIZE)
    new_states = []
    for par, gain in enumerate(gains):
        keep = low_half if par == 0 else jnp.logical_not(low_half)
        qm = jnp.where(keep, q, jnp.zeros_like(q))
        s = lax.dot_general(qm, k, (((1,), (1,)), ((), ())), preferred_element_type=jnp.float32)
        s = s * scale + gain
        m = jnp.max(s, axis=1, keepdims=True)
        p = jnp.exp(s - m).astype(jnp.bfloat16)
        d = jnp.sum(p.astype(jnp.float32), axis=1, keepdims=True)
        n = jnp.dot(p, v, preferred_element_type=jnp.float32)
        if states is None:
            new_states.append((m, n, d))
        else:
            ma, na, da = states[par]
            mx = jnp.maximum(ma, m)
            sa = jnp.exp(ma - mx)
            sb = jnp.exp(m - mx)
            new_states.append((mx, na * sa + n * sb, da * sa + d * sb))
    return new_states


def near_kernel(q0_ref, k0_ref, v0_ref, fq_ref, fkv_ref, gain_ref, m_ref, n_ref, d_ref, qw_ref):
    tokens, width_all = q0_ref.shape
    head_count = width_all // HEAD_SIZE
    widen_queries(fq_ref, qw_ref, 1)
    lane = lax.broadcasted_iota(jnp.int32, (1, LANE_BLOCK), 1)
    low_half = lane < HEAD_SIZE

    def block_body(j, carry):
        off = pl.multiple_of(j * LANE_BLOCK, LANE_BLOCK)
        head = j * 2
        states = None
        for level in range(fq_ref.shape[0] + 1):
            if level == 0:
                q = q0_ref[:, pl.ds(off, LANE_BLOCK)]
                k = k0_ref[:, pl.ds(off, LANE_BLOCK)]
                v = v0_ref[:, pl.ds(off, LANE_BLOCK)]
            else:
                q = qw_ref[level - 1, :, pl.ds(off, LANE_BLOCK)]
                k = fkv_ref[level - 1, :, pl.ds(off, LANE_BLOCK)]
                v = fkv_ref[level - 1, :, pl.ds(off + width_all, LANE_BLOCK)]
            gains = [gain_ref[level * head_count + head + par] for par in range(2)]
            states = level_step(states, q, k, v, gains, low_half)
        shape = (tokens, LANE_BLOCK)
        m_ref[:, pl.ds(off, LANE_BLOCK)] = jnp.where(
            low_half, jnp.broadcast_to(states[0][0], shape), jnp.broadcast_to(states[1][0], shape)
        )
        n_ref[:, pl.ds(off, LANE_BLOCK)] = jnp.where(low_half, states[0][1], states[1][1])
        d_ref[:, pl.ds(off, LANE_BLOCK)] = jnp.where(
            low_half, jnp.broadcast_to(states[0][2], shape), jnp.broadcast_to(states[1][2], shape)
        )
        return carry

    lax.fori_loop(0, width_all // LANE_BLOCK, block_body, 0)


def far_kernel(first_level, senders, *refs):
    m_ref, n_ref, d_ref, fq_ref = refs[:4]
    msg_refs = refs[4:4 + senders]
    gain_ref, w_ref, out_ref, qw_ref, kv_ref, acc_ref = refs[4 + senders:]
    tokens, width_all = n_ref.shape
    head_count = width_all // HEAD_SIZE
    far_count = fq_ref.shape[0]
    col_rows = msg_refs[0].shape[0] // far_count
    for b in range(far_count):
        for s in range(senders):
            kv_ref[b, s * col_rows:(s + 1) * col_rows, :] = msg_refs[s][
                b * col_rows:(b + 1) * col_rows, :
            ]
    widen_queries(fq_ref, qw_ref, first_level)
    lane = lax.broadcasted_iota(jnp.int32, (1, LANE_BLOCK), 1)
    low_half = lane < HEAD_SIZE
    at_zero = lane == 0
    at_half = lane == HEAD_SIZE

    def block_body(j, carry):
        off = pl.multiple_of(j * LANE_BLOCK, LANE_BLOCK)
        head = j * 2
        m_blk = m_ref[:, pl.ds(off, LANE_BLOCK)]
        n_blk = n_ref[:, pl.ds(off, LANE_BLOCK)]
        d_blk = d_ref[:, pl.ds(off, LANE_BLOCK)]
        states = []
        for pick in (at_zero, at_half):
            m0 = jnp.max(jnp.where(pick, m_blk, -jnp.inf), axis=1, keepdims=True)
            d0 = jnp.sum(jnp.where(pick, d_blk, 0.0), axis=1, keepdims=True)
            states.append((m0, n_blk, d0))
        for i in range(far_count):
            level = first_level + i
            q = qw_ref[i, :, pl.ds(off, LANE_BLOCK)]
            k = kv_ref[i, :, pl.ds(off, LANE_BLOCK)]
            v = kv_ref[i, :, pl.ds(off + width_all, LANE_BLOCK)]
            gains = [gain_ref[level * head_count + head + par] for par in range(2)]
            states = level_step(states, q, k, v, gains, low_half)
        out_lo = states[0][1] / states[0][2]
        out_hi = states[1][1] / states[1][2]
        acc_ref[:, pl.ds(off, LANE_BLOCK)] = jnp.where(low_half, out_lo, out_hi).astype(
            jnp.bfloat16
        )
        return carry

    lax.fori_loop(0, width_all // LANE_BLOCK, block_body, 0)
    out_ref[...] = jnp.dot(acc_ref[...], w_ref[...], preferred_element_type=jnp.float32).astype(
        out_ref.dtype
    )


VMEM_SPEC = pl.BlockSpec(memory_space=pltpu.VMEM)
SMEM_SPEC = pl.BlockSpec(memory_space=pltpu.SMEM)


def near_attention(q0, k0, v0, near_q, near_kv, level_gain):
    tokens, width_all = q0.shape
    state = jax.ShapeDtypeStruct((tokens, width_all), jnp.float32)
    return pl.pallas_call(
        near_kernel,
        out_shape=(state, state, state),
        in_specs=[VMEM_SPEC] * 5 + [SMEM_SPEC],
        out_specs=(VMEM_SPEC, VMEM_SPEC, VMEM_SPEC),
        scratch_shapes=[pltpu.VMEM((near_q.shape[0], tokens, width_all), jnp.bfloat16)],
    )(q0, k0, v0, near_q, near_kv, level_gain)


def far_attention(first_level, m_st, n_st, d_st, far_q, messages, level_gain, weight):
    tokens, width_all = n_st.shape
    far_count = far_q.shape[0]
    return pl.pallas_call(
        functools.partial(far_kernel, first_level, len(messages)),
        out_shape=jax.ShapeDtypeStruct((tokens, width_all), jnp.bfloat16),
        in_specs=[VMEM_SPEC] * (4 + len(messages)) + [SMEM_SPEC, VMEM_SPEC],
        out_specs=VMEM_SPEC,
        scratch_shapes=[
            pltpu.VMEM((far_count, tokens, width_all), jnp.bfloat16),
            pltpu.VMEM((far_count, BLOCK, 2 * width_all), jnp.bfloat16),
            pltpu.VMEM((tokens, width_all), jnp.bfloat16),
        ],
    )(m_st, n_st, d_st, far_q, *messages, level_gain, weight)


def xor_pairs(size, bit):
    return [(i, i ^ bit) for i in range(size)]


def on_device(query_rows, key_rows, value_rows, distance_slope, out_weight):
    tokens, width_all = query_rows.shape
    head_count = distance_slope.shape[0]
    head_size = width_all // head_count
    fine_size = lax.axis_size("fine")
    coarse_size = lax.axis_size("coarse")
    local_levels = (tokens // BLOCK).bit_length() - 1
    fine_bits = fine_size.bit_length() - 1
    coarse_bits = coarse_size.bit_length() - 1
    level_total = local_levels + fine_bits + coarse_bits
    first_fine = local_levels
    first_coarse = local_levels + fine_bits
    slope_term = LOG_TWO * (1.0 - distance_slope)

    full_weight = lax.all_gather(out_weight, "coarse", axis=0, tiled=True)

    pyramid = [jnp.concatenate([query_rows, key_rows, value_rows], axis=1)]
    for _ in range(1, level_total):
        pyramid.append(coarsen(pyramid[-1]))

    def kv_of(level):
        return pyramid[level][:, width_all:]

    column = {m: kv_of(m) for m in range(first_coarse, level_total)}
    sibling_cols = []
    for bit_no in range(coarse_bits):
        level_now = first_coarse + bit_no
        pending = list(range(level_now, level_total))
        sizes = [column[m].shape[0] for m in pending]
        message = jnp.concatenate([column[m] for m in pending], axis=0)
        received = lax.ppermute(message, "coarse", xor_pairs(coarse_size, 1 << bit_no))
        offsets = np.cumsum([0] + sizes)
        for i, m in enumerate(pending):
            got = received[offsets[i]:offsets[i + 1]]
            if m == level_now:
                sibling_cols.append(got)
            else:
                column[m] = jnp.concatenate([column[m], got], axis=0)

    fine_keys = {l: [] for l in range(first_fine, first_coarse)}
    for offset in range(1, fine_size):
        level_now = first_fine + offset.bit_length() - 1
        fine_keys[level_now].append(
            lax.ppermute(kv_of(level_now), "fine", xor_pairs(fine_size, offset))
        )

    coarse_msg = jnp.concatenate(sibling_cols, axis=0)
    fine_msgs = [coarse_msg]
    for offset in range(1, fine_size):
        fine_msgs.append(lax.ppermute(coarse_msg, "fine", xor_pairs(fine_size, offset)))
    level_gain = jnp.concatenate([l * slope_term for l in range(level_total)])

    def padded_queries(levels):
        return jnp.stack(
            [
                jnp.pad(pyramid[l][:, :width_all], ((0, BLOCK - pyramid[l].shape[0]), (0, 0)))
                for l in levels
            ]
        )

    near_levels = list(range(first_fine, first_coarse))
    near_kv = jnp.stack([jnp.concatenate(fine_keys[l], axis=0) for l in near_levels])
    m_st, n_st, d_st = near_attention(
        query_rows, key_rows, value_rows, padded_queries(near_levels), near_kv, level_gain
    )
    return far_attention(
        first_coarse,
        m_st,
        n_st,
        d_st,
        padded_queries(list(range(first_coarse, level_total))),
        fine_msgs,
        level_gain,
        full_weight,
    )


def solution(mesh):
    return jax.shard_map(
        on_device,
        mesh=mesh,
        in_specs=(
            P(("coarse", "fine"), None),
            P(("coarse", "fine"), None),
            P(("coarse", "fine"), None),
            P(),
            P("coarse", None),
        ),
        out_specs=P(("coarse", "fine"), None),
        check_vma=False,
    )
```

```python
import functools
import math

import jax
import jax.numpy as jnp
import numpy as np
from jax import lax
from jax.experimental import pallas as pl
from jax.experimental.pallas import tpu as pltpu
from jax.sharding import PartitionSpec as P

BLOCK = 128


LOG_TWO = math.log(2.0)


def coarsen(row_data):
    dims_all = row_data.shape
    paired = row_data.reshape(dims_all[:-2] + (dims_all[-2] // 2, 2, dims_all[-1])).astype(
        jnp.float32
    )
    return ((paired[..., 0, :] + paired[..., 1, :]) * 0.5).astype(jnp.bfloat16)


HEAD_SIZE = 64
LANE_BLOCK = 128


def widen_queries(fq_ref, qw_ref, first_level):
    tokens = qw_ref.shape[1]
    rows = lax.broadcasted_iota(jnp.int32, (tokens, BLOCK), 0)
    cols = lax.broadcasted_iota(jnp.int32, (tokens, BLOCK), 1)
    for i in range(fq_ref.shape[0]):
        spread = ((rows >> (first_level + i)) == cols).astype(jnp.bfloat16)
        qw_ref[i] = jnp.dot(spread, fq_ref[i], preferred_element_type=jnp.float32).astype(
            jnp.bfloat16
        )


def level_step(states, q, k, v, gains, low_half):
    scale = 1.0 / math.sqrt(HEAD_SIZE)
    new_states = []
    for par, gain in enumerate(gains):
        keep = low_half if par == 0 else jnp.logical_not(low_half)
        qm = jnp.where(keep, q, jnp.zeros_like(q))
        s = lax.dot_general(qm, k, (((1,), (1,)), ((), ())), preferred_element_type=jnp.float32)
        s = s * scale + gain
        m = jnp.max(s, axis=1, keepdims=True)
        p = jnp.exp(s - m).astype(jnp.bfloat16)
        d = jnp.sum(p.astype(jnp.float32), axis=1, keepdims=True)
        n = jnp.dot(p, v, preferred_element_type=jnp.float32)
        if states is None:
            new_states.append((m, n, d))
        else:
            ma, na, da = states[par]
            mx = jnp.maximum(ma, m)
            sa = jnp.exp(ma - mx)
            sb = jnp.exp(m - mx)
            new_states.append((mx, na * sa + n * sb, da * sa + d * sb))
    return new_states


def near_kernel(q0_ref, k0_ref, v0_ref, fq_ref, fkv_ref, gain_ref, m_ref, n_ref, d_ref, qw_ref):
    tokens, width_all = q0_ref.shape
    head_count = width_all // HEAD_SIZE
    widen_queries(fq_ref, qw_ref, 1)
    lane = lax.broadcasted_iota(jnp.int32, (1, LANE_BLOCK), 1)
    low_half = lane < HEAD_SIZE

    def block_body(j, carry):
        off = pl.multiple_of(j * LANE_BLOCK, LANE_BLOCK)
        head = j * 2
        states = None
        for level in range(fq_ref.shape[0] + 1):
            if level == 0:
                q = q0_ref[:, pl.ds(off, LANE_BLOCK)]
                k = k0_ref[:, pl.ds(off, LANE_BLOCK)]
                v = v0_ref[:, pl.ds(off, LANE_BLOCK)]
            else:
                q = qw_ref[level - 1, :, pl.ds(off, LANE_BLOCK)]
                k = fkv_ref[level - 1, :, pl.ds(off, LANE_BLOCK)]
                v = fkv_ref[level - 1, :, pl.ds(off + width_all, LANE_BLOCK)]
            gains = [gain_ref[level * head_count + head + par] for par in range(2)]
            states = level_step(states, q, k, v, gains, low_half)
        shape = (tokens, LANE_BLOCK)
        m_ref[:, pl.ds(off, LANE_BLOCK)] = jnp.where(
            low_half, jnp.broadcast_to(states[0][0], shape), jnp.broadcast_to(states[1][0], shape)
        )
        n_ref[:, pl.ds(off, LANE_BLOCK)] = jnp.where(low_half, states[0][1], states[1][1])
        d_ref[:, pl.ds(off, LANE_BLOCK)] = jnp.where(
            low_half, jnp.broadcast_to(states[0][2], shape), jnp.broadcast_to(states[1][2], shape)
        )
        return carry

    lax.fori_loop(0, width_all // LANE_BLOCK, block_body, 0)


def far_kernel(first_level, senders, *refs):
    m_ref, n_ref, d_ref, fq_ref = refs[:4]
    msg_refs = refs[4:4 + senders]
    gain_ref, w_ref, out_ref, qw_ref, kv_ref, acc_ref = refs[4 + senders:]
    tokens, width_all = n_ref.shape
    head_count = width_all // HEAD_SIZE
    far_count = fq_ref.shape[0]
    col_rows = msg_refs[0].shape[0] // far_count
    for b in range(far_count):
        for s in range(senders):
            kv_ref[b, s * col_rows:(s + 1) * col_rows, :] = msg_refs[s][
                b * col_rows:(b + 1) * col_rows, :
            ]
    widen_queries(fq_ref, qw_ref, first_level)
    lane = lax.broadcasted_iota(jnp.int32, (1, LANE_BLOCK), 1)
    low_half = lane < HEAD_SIZE
    at_zero = lane == 0
    at_half = lane == HEAD_SIZE

    def block_body(j, carry):
        off = pl.multiple_of(j * LANE_BLOCK, LANE_BLOCK)
        head = j * 2
        m_blk = m_ref[:, pl.ds(off, LANE_BLOCK)]
        n_blk = n_ref[:, pl.ds(off, LANE_BLOCK)]
        d_blk = d_ref[:, pl.ds(off, LANE_BLOCK)]
        states = []
        for pick in (at_zero, at_half):
            m0 = jnp.max(jnp.where(pick, m_blk, -jnp.inf), axis=1, keepdims=True)
            d0 = jnp.sum(jnp.where(pick, d_blk, 0.0), axis=1, keepdims=True)
            states.append((m0, n_blk, d0))
        for i in range(far_count):
            level = first_level + i
            q = qw_ref[i, :, pl.ds(off, LANE_BLOCK)]
            k = kv_ref[i, :, pl.ds(off, LANE_BLOCK)]
            v = kv_ref[i, :, pl.ds(off + width_all, LANE_BLOCK)]
            gains = [gain_ref[level * head_count + head + par] for par in range(2)]
            states = level_step(states, q, k, v, gains, low_half)
        out_lo = states[0][1] / states[0][2]
        out_hi = states[1][1] / states[1][2]
        acc_ref[:, pl.ds(off, LANE_BLOCK)] = jnp.where(low_half, out_lo, out_hi).astype(
            jnp.bfloat16
        )
        return carry

    lax.fori_loop(0, width_all // LANE_BLOCK, block_body, 0)
    out_ref[...] = jnp.dot(acc_ref[...], w_ref[...], preferred_element_type=jnp.float32).astype(
        out_ref.dtype
    )


VMEM_SPEC = pl.BlockSpec(memory_space=pltpu.VMEM)
SMEM_SPEC = pl.BlockSpec(memory_space=pltpu.SMEM)


def near_attention(q0, k0, v0, near_q, near_kv, level_gain):
    tokens, width_all = q0.shape
    state = jax.ShapeDtypeStruct((tokens, width_all), jnp.float32)
    return pl.pallas_call(
        near_kernel,
        out_shape=(state, state, state),
        in_specs=[VMEM_SPEC] * 5 + [SMEM_SPEC],
        out_specs=(VMEM_SPEC, VMEM_SPEC, VMEM_SPEC),
        scratch_shapes=[pltpu.VMEM((near_q.shape[0], tokens, width_all), jnp.bfloat16)],
    )(q0, k0, v0, near_q, near_kv, level_gain)


def far_attention(first_level, m_st, n_st, d_st, far_q, messages, level_gain, weight):
    tokens, width_all = n_st.shape
    far_count = far_q.shape[0]
    return pl.pallas_call(
        functools.partial(far_kernel, first_level, len(messages)),
        out_shape=jax.ShapeDtypeStruct((tokens, width_all), jnp.bfloat16),
        in_specs=[VMEM_SPEC] * (4 + len(messages)) + [SMEM_SPEC, VMEM_SPEC],
        out_specs=VMEM_SPEC,
        scratch_shapes=[
            pltpu.VMEM((far_count, tokens, width_all), jnp.bfloat16),
            pltpu.VMEM((far_count, BLOCK, 2 * width_all), jnp.bfloat16),
            pltpu.VMEM((tokens, width_all), jnp.bfloat16),
        ],
    )(m_st, n_st, d_st, far_q, *messages, level_gain, weight)


def xor_pairs(size, bit):
    return [(i, i ^ bit) for i in range(size)]


def on_device(query_rows, key_rows, value_rows, distance_slope, out_weight):
    tokens, width_all = query_rows.shape
    head_count = distance_slope.shape[0]
    head_size = width_all // head_count
    fine_size = lax.axis_size("fine")
    coarse_size = lax.axis_size("coarse")
    local_levels = (tokens // BLOCK).bit_length() - 1
    fine_bits = fine_size.bit_length() - 1
    coarse_bits = coarse_size.bit_length() - 1
    level_total = local_levels + fine_bits + coarse_bits
    first_fine = local_levels
    first_coarse = local_levels + fine_bits
    slope_term = LOG_TWO * (1.0 - distance_slope)

    coarse_index = lax.axis_index("coarse")

    pyramid = [jnp.concatenate([query_rows, key_rows, value_rows], axis=1)]
    for _ in range(1, level_total):
        pyramid.append(coarsen(pyramid[-1]))

    def kv_of(level):
        return pyramid[level][:, width_all:]

    column = {m: kv_of(m) for m in range(first_coarse, level_total)}
    sibling_cols = []
    for bit_no in range(coarse_bits):
        level_now = first_coarse + bit_no
        pending = list(range(level_now, level_total))
        sizes = [column[m].shape[0] for m in pending]
        message = jnp.concatenate([column[m] for m in pending], axis=0)
        received = lax.ppermute(message, "coarse", xor_pairs(coarse_size, 1 << bit_no))
        offsets = np.cumsum([0] + sizes)
        for i, m in enumerate(pending):
            got = received[offsets[i]:offsets[i + 1]]
            if m == level_now:
                sibling_cols.append(got)
            else:
                column[m] = jnp.concatenate([column[m], got], axis=0)

    full_weight = out_weight
    for bit_no in range(coarse_bits):
        got = lax.ppermute(full_weight, "coarse", xor_pairs(coarse_size, 1 << bit_no))
        upper = ((coarse_index >> bit_no) & 1) == 1
        full_weight = jnp.where(
            upper,
            jnp.concatenate([got, full_weight], axis=0),
            jnp.concatenate([full_weight, got], axis=0),
        )

    fine_keys = {l: [] for l in range(first_fine, first_coarse)}
    for offset in range(1, fine_size):
        level_now = first_fine + offset.bit_length() - 1
        fine_keys[level_now].append(
            lax.ppermute(kv_of(level_now), "fine", xor_pairs(fine_size, offset))
        )

    coarse_msg = jnp.concatenate(sibling_cols, axis=0)
    fine_msgs = [coarse_msg]
    for offset in range(1, fine_size):
        fine_msgs.append(lax.ppermute(coarse_msg, "fine", xor_pairs(fine_size, offset)))
    level_gain = jnp.concatenate([l * slope_term for l in range(level_total)])

    def padded_queries(levels):
        return jnp.stack(
            [
                jnp.pad(pyramid[l][:, :width_all], ((0, BLOCK - pyramid[l].shape[0]), (0, 0)))
                for l in levels
            ]
        )

    near_levels = list(range(first_fine, first_coarse))
    near_kv = jnp.stack([jnp.concatenate(fine_keys[l], axis=0) for l in near_levels])
    m_st, n_st, d_st = near_attention(
        query_rows, key_rows, value_rows, padded_queries(near_levels), near_kv, level_gain
    )
    return far_attention(
        first_coarse,
        m_st,
        n_st,
        d_st,
        padded_queries(list(range(first_coarse, level_total))),
        fine_msgs,
        level_gain,
        full_weight,
    )


def solution(mesh):
    return jax.shard_map(
        on_device,
        mesh=mesh,
        in_specs=(
            P(("coarse", "fine"), None),
            P(("coarse", "fine"), None),
            P(("coarse", "fine"), None),
            P(),
            P("coarse", None),
        ),
        out_specs=P(("coarse", "fine"), None),
        check_vma=False,
    )
```

```python
import functools
import math

import jax
import jax.numpy as jnp
import numpy as np
from jax import lax
from jax.experimental import pallas as pl
from jax.experimental.pallas import tpu as pltpu
from jax.sharding import PartitionSpec as P

BLOCK = 128


LOG_TWO = math.log(2.0)


def coarsen(row_data):
    dims_all = row_data.shape
    paired = row_data.reshape(dims_all[:-2] + (dims_all[-2] // 2, 2, dims_all[-1])).astype(
        jnp.float32
    )
    return ((paired[..., 0, :] + paired[..., 1, :]) * 0.5).astype(jnp.bfloat16)


HEAD_SIZE = 64
LANE_BLOCK = 128


def widen_queries(fq_ref, qw_ref, first_level):
    tokens = qw_ref.shape[1]
    rows = lax.broadcasted_iota(jnp.int32, (tokens, BLOCK), 0)
    cols = lax.broadcasted_iota(jnp.int32, (tokens, BLOCK), 1)
    for i in range(fq_ref.shape[0]):
        spread = ((rows >> (first_level + i)) == cols).astype(jnp.bfloat16)
        qw_ref[i] = jnp.dot(spread, fq_ref[i], preferred_element_type=jnp.float32).astype(
            jnp.bfloat16
        )


def level_step(states, q, k, v, gains, low_half):
    scale = 1.0 / math.sqrt(HEAD_SIZE)
    new_states = []
    for par, gain in enumerate(gains):
        keep = low_half if par == 0 else jnp.logical_not(low_half)
        qm = jnp.where(keep, q, jnp.zeros_like(q))
        s = lax.dot_general(qm, k, (((1,), (1,)), ((), ())), preferred_element_type=jnp.float32)
        s = s * scale + gain
        m = jnp.max(s, axis=1, keepdims=True)
        p = jnp.exp(s - m).astype(jnp.bfloat16)
        d = jnp.sum(p.astype(jnp.float32), axis=1, keepdims=True)
        n = jnp.dot(p, v, preferred_element_type=jnp.float32)
        if states is None:
            new_states.append((m, n, d))
        else:
            ma, na, da = states[par]
            mx = jnp.maximum(ma, m)
            sa = jnp.exp(ma - mx)
            sb = jnp.exp(m - mx)
            new_states.append((mx, na * sa + n * sb, da * sa + d * sb))
    return new_states


def near_kernel(q0_ref, k0_ref, v0_ref, fq_ref, fkv_ref, gain_ref, m_ref, n_ref, d_ref, qw_ref):
    tokens, width_all = q0_ref.shape
    head_count = width_all // HEAD_SIZE
    widen_queries(fq_ref, qw_ref, 1)
    lane = lax.broadcasted_iota(jnp.int32, (1, LANE_BLOCK), 1)
    low_half = lane < HEAD_SIZE

    def block_body(j, carry):
        off = pl.multiple_of(j * LANE_BLOCK, LANE_BLOCK)
        head = j * 2
        states = None
        for level in range(fq_ref.shape[0] + 1):
            if level == 0:
                q = q0_ref[:, pl.ds(off, LANE_BLOCK)]
                k = k0_ref[:, pl.ds(off, LANE_BLOCK)]
                v = v0_ref[:, pl.ds(off, LANE_BLOCK)]
            else:
                q = qw_ref[level - 1, :, pl.ds(off, LANE_BLOCK)]
                k = fkv_ref[level - 1, :, pl.ds(off, LANE_BLOCK)]
                v = fkv_ref[level - 1, :, pl.ds(off + width_all, LANE_BLOCK)]
            gains = [gain_ref[level * head_count + head + par] for par in range(2)]
            states = level_step(states, q, k, v, gains, low_half)
        shape = (tokens, LANE_BLOCK)
        m_ref[:, pl.ds(off, LANE_BLOCK)] = jnp.where(
            low_half, jnp.broadcast_to(states[0][0], shape), jnp.broadcast_to(states[1][0], shape)
        )
        n_ref[:, pl.ds(off, LANE_BLOCK)] = jnp.where(low_half, states[0][1], states[1][1])
        d_ref[:, pl.ds(off, LANE_BLOCK)] = jnp.where(
            low_half, jnp.broadcast_to(states[0][2], shape), jnp.broadcast_to(states[1][2], shape)
        )
        return carry

    lax.fori_loop(0, width_all // LANE_BLOCK, block_body, 0)


def far_kernel(first_level, senders, *refs):
    m_ref, n_ref, d_ref, fq_ref = refs[:4]
    msg_refs = refs[4:4 + senders]
    gain_ref, w_ref, out_ref, qw_ref, kv_ref, acc_ref = refs[4 + senders:]
    tokens, width_all = n_ref.shape
    head_count = width_all // HEAD_SIZE
    far_count = fq_ref.shape[0]
    col_rows = msg_refs[0].shape[0] // far_count
    for b in range(far_count):
        for s in range(senders):
            kv_ref[b, s * col_rows:(s + 1) * col_rows, :] = msg_refs[s][
                b * col_rows:(b + 1) * col_rows, :
            ]
    widen_queries(fq_ref, qw_ref, first_level)
    lane = lax.broadcasted_iota(jnp.int32, (1, LANE_BLOCK), 1)
    low_half = lane < HEAD_SIZE
    at_zero = lane == 0
    at_half = lane == HEAD_SIZE

    def block_body(j, carry):
        off = pl.multiple_of(j * LANE_BLOCK, LANE_BLOCK)
        head = j * 2
        m_blk = m_ref[:, pl.ds(off, LANE_BLOCK)]
        n_blk = n_ref[:, pl.ds(off, LANE_BLOCK)]
        d_blk = d_ref[:, pl.ds(off, LANE_BLOCK)]
        states = []
        for pick in (at_zero, at_half):
            m0 = jnp.max(jnp.where(pick, m_blk, -jnp.inf), axis=1, keepdims=True)
            d0 = jnp.sum(jnp.where(pick, d_blk, 0.0), axis=1, keepdims=True)
            states.append((m0, n_blk, d0))
        for i in range(far_count):
            level = first_level + i
            q = qw_ref[i, :, pl.ds(off, LANE_BLOCK)]
            k = kv_ref[i, :, pl.ds(off, LANE_BLOCK)]
            v = kv_ref[i, :, pl.ds(off + width_all, LANE_BLOCK)]
            gains = [gain_ref[level * head_count + head + par] for par in range(2)]
            states = level_step(states, q, k, v, gains, low_half)
        out_lo = states[0][1] / states[0][2]
        out_hi = states[1][1] / states[1][2]
        acc_ref[:, pl.ds(off, LANE_BLOCK)] = jnp.where(low_half, out_lo, out_hi).astype(
            jnp.bfloat16
        )
        return carry

    lax.fori_loop(0, width_all // LANE_BLOCK, block_body, 0)
    out_ref[...] = jnp.dot(acc_ref[...], w_ref[...], preferred_element_type=jnp.float32).astype(
        out_ref.dtype
    )


VMEM_SPEC = pl.BlockSpec(memory_space=pltpu.VMEM)
SMEM_SPEC = pl.BlockSpec(memory_space=pltpu.SMEM)


def near_attention(q0, k0, v0, near_q, near_kv, level_gain):
    tokens, width_all = q0.shape
    state = jax.ShapeDtypeStruct((tokens, width_all), jnp.float32)
    return pl.pallas_call(
        near_kernel,
        out_shape=(state, state, state),
        in_specs=[VMEM_SPEC] * 5 + [SMEM_SPEC],
        out_specs=(VMEM_SPEC, VMEM_SPEC, VMEM_SPEC),
        scratch_shapes=[pltpu.VMEM((near_q.shape[0], tokens, width_all), jnp.bfloat16)],
    )(q0, k0, v0, near_q, near_kv, level_gain)


def far_attention(first_level, m_st, n_st, d_st, far_q, messages, level_gain, weight):
    tokens, width_all = n_st.shape
    far_count = far_q.shape[0]
    return pl.pallas_call(
        functools.partial(far_kernel, first_level, len(messages)),
        out_shape=jax.ShapeDtypeStruct((tokens, width_all), jnp.bfloat16),
        in_specs=[VMEM_SPEC] * (4 + len(messages)) + [SMEM_SPEC, VMEM_SPEC],
        out_specs=VMEM_SPEC,
        scratch_shapes=[
            pltpu.VMEM((far_count, tokens, width_all), jnp.bfloat16),
            pltpu.VMEM((far_count, BLOCK, 2 * width_all), jnp.bfloat16),
            pltpu.VMEM((tokens, width_all), jnp.bfloat16),
        ],
    )(m_st, n_st, d_st, far_q, *messages, level_gain, weight)


def xor_pairs(size, bit):
    return [(i, i ^ bit) for i in range(size)]


def on_device(query_rows, key_rows, value_rows, distance_slope, out_weight):
    tokens, width_all = query_rows.shape
    head_count = distance_slope.shape[0]
    head_size = width_all // head_count
    fine_size = lax.axis_size("fine")
    coarse_size = lax.axis_size("coarse")
    local_levels = (tokens // BLOCK).bit_length() - 1
    fine_bits = fine_size.bit_length() - 1
    coarse_bits = coarse_size.bit_length() - 1
    level_total = local_levels + fine_bits + coarse_bits
    first_fine = local_levels
    first_coarse = local_levels + fine_bits
    slope_term = LOG_TWO * (1.0 - distance_slope)

    fine_index = lax.axis_index("fine")
    weight_rows = out_weight.shape[0] // fine_size
    full_weight = lax.all_gather(
        lax.dynamic_slice_in_dim(out_weight, fine_index * weight_rows, weight_rows, axis=0),
        ("coarse", "fine"),
        axis=0,
        tiled=True,
    )

    pyramid = [jnp.concatenate([query_rows, key_rows, value_rows], axis=1)]
    for _ in range(1, level_total):
        pyramid.append(coarsen(pyramid[-1]))

    def kv_of(level):
        return pyramid[level][:, width_all:]

    column = {m: kv_of(m) for m in range(first_coarse, level_total)}
    sibling_cols = []
    for bit_no in range(coarse_bits):
        level_now = first_coarse + bit_no
        pending = list(range(level_now, level_total))
        sizes = [column[m].shape[0] for m in pending]
        message = jnp.concatenate([column[m] for m in pending], axis=0)
        received = lax.ppermute(message, "coarse", xor_pairs(coarse_size, 1 << bit_no))
        offsets = np.cumsum([0] + sizes)
        for i, m in enumerate(pending):
            got = received[offsets[i]:offsets[i + 1]]
            if m == level_now:
                sibling_cols.append(got)
            else:
                column[m] = jnp.concatenate([column[m], got], axis=0)

    fine_keys = {l: [] for l in range(first_fine, first_coarse)}
    for offset in range(1, fine_size):
        level_now = first_fine + offset.bit_length() - 1
        fine_keys[level_now].append(
            lax.ppermute(kv_of(level_now), "fine", xor_pairs(fine_size, offset))
        )

    coarse_msg = jnp.concatenate(sibling_cols, axis=0)
    fine_msgs = [coarse_msg]
    for offset in range(1, fine_size):
        fine_msgs.append(lax.ppermute(coarse_msg, "fine", xor_pairs(fine_size, offset)))
    level_gain = jnp.concatenate([l * slope_term for l in range(level_total)])

    def padded_queries(levels):
        return jnp.stack(
            [
                jnp.pad(pyramid[l][:, :width_all], ((0, BLOCK - pyramid[l].shape[0]), (0, 0)))
                for l in levels
            ]
        )

    near_levels = list(range(first_fine, first_coarse))
    near_kv = jnp.stack([jnp.concatenate(fine_keys[l], axis=0) for l in near_levels])
    m_st, n_st, d_st = near_attention(
        query_rows, key_rows, value_rows, padded_queries(near_levels), near_kv, level_gain
    )
    return far_attention(
        first_coarse,
        m_st,
        n_st,
        d_st,
        padded_queries(list(range(first_coarse, level_total))),
        fine_msgs,
        level_gain,
        full_weight,
    )


def solution(mesh):
    return jax.shard_map(
        on_device,
        mesh=mesh,
        in_specs=(
            P(("coarse", "fine"), None),
            P(("coarse", "fine"), None),
            P(("coarse", "fine"), None),
            P(),
            P("coarse", None),
        ),
        out_specs=P(("coarse", "fine"), None),
        check_vma=False,
    )
```

```python
import functools
import math

import jax
import jax.numpy as jnp
import numpy as np
from jax import lax
from jax.experimental import pallas as pl
from jax.experimental.pallas import tpu as pltpu
from jax.sharding import PartitionSpec as P

BLOCK = 128


LOG_TWO = math.log(2.0)


def coarsen(row_data):
    dims_all = row_data.shape
    paired = row_data.reshape(dims_all[:-2] + (dims_all[-2] // 2, 2, dims_all[-1])).astype(
        jnp.float32
    )
    return ((paired[..., 0, :] + paired[..., 1, :]) * 0.5).astype(jnp.bfloat16)


HEAD_SIZE = 64
LANE_BLOCK = 128


def widen_queries(fq_ref, qw_ref, first_level):
    tokens = qw_ref.shape[1]
    rows = lax.broadcasted_iota(jnp.int32, (tokens, BLOCK), 0)
    cols = lax.broadcasted_iota(jnp.int32, (tokens, BLOCK), 1)
    for i in range(fq_ref.shape[0]):
        spread = ((rows >> (first_level + i)) == cols).astype(jnp.bfloat16)
        qw_ref[i] = jnp.dot(spread, fq_ref[i], preferred_element_type=jnp.float32).astype(
            jnp.bfloat16
        )


def level_step(states, q, k, v, gains, low_half):
    scale = 1.0 / math.sqrt(HEAD_SIZE)
    new_states = []
    for par, gain in enumerate(gains):
        keep = low_half if par == 0 else jnp.logical_not(low_half)
        qm = jnp.where(keep, q, jnp.zeros_like(q))
        s = lax.dot_general(qm, k, (((1,), (1,)), ((), ())), preferred_element_type=jnp.float32)
        s = s * scale + gain
        m = jnp.max(s, axis=1, keepdims=True)
        p = jnp.exp(s - m).astype(jnp.bfloat16)
        d = jnp.sum(p.astype(jnp.float32), axis=1, keepdims=True)
        n = jnp.dot(p, v, preferred_element_type=jnp.float32)
        if states is None:
            new_states.append((m, n, d))
        else:
            ma, na, da = states[par]
            mx = jnp.maximum(ma, m)
            sa = jnp.exp(ma - mx)
            sb = jnp.exp(m - mx)
            new_states.append((mx, na * sa + n * sb, da * sa + d * sb))
    return new_states


def near_kernel(q0_ref, k0_ref, v0_ref, fq_ref, fkv_ref, gain_ref, m_ref, n_ref, d_ref, qw_ref):
    tokens, width_all = q0_ref.shape
    head_count = width_all // HEAD_SIZE
    widen_queries(fq_ref, qw_ref, 1)
    lane = lax.broadcasted_iota(jnp.int32, (1, LANE_BLOCK), 1)
    low_half = lane < HEAD_SIZE

    def block_body(j, carry):
        off = pl.multiple_of(j * LANE_BLOCK, LANE_BLOCK)
        head = j * 2
        states = None
        for level in range(fq_ref.shape[0] + 1):
            if level == 0:
                q = q0_ref[:, pl.ds(off, LANE_BLOCK)]
                k = k0_ref[:, pl.ds(off, LANE_BLOCK)]
                v = v0_ref[:, pl.ds(off, LANE_BLOCK)]
            else:
                q = qw_ref[level - 1, :, pl.ds(off, LANE_BLOCK)]
                k = fkv_ref[level - 1, :, pl.ds(off, LANE_BLOCK)]
                v = fkv_ref[level - 1, :, pl.ds(off + width_all, LANE_BLOCK)]
            gains = [gain_ref[level * head_count + head + par] for par in range(2)]
            states = level_step(states, q, k, v, gains, low_half)
        shape = (tokens, LANE_BLOCK)
        m_ref[:, pl.ds(off, LANE_BLOCK)] = jnp.where(
            low_half, jnp.broadcast_to(states[0][0], shape), jnp.broadcast_to(states[1][0], shape)
        )
        n_ref[:, pl.ds(off, LANE_BLOCK)] = jnp.where(low_half, states[0][1], states[1][1])
        d_ref[:, pl.ds(off, LANE_BLOCK)] = jnp.where(
            low_half, jnp.broadcast_to(states[0][2], shape), jnp.broadcast_to(states[1][2], shape)
        )
        return carry

    lax.fori_loop(0, width_all // LANE_BLOCK, block_body, 0)


def far_kernel(first_level, senders, *refs):
    m_ref, n_ref, d_ref, fq_ref = refs[:4]
    msg_refs = refs[4:4 + senders]
    gain_ref, w_ref, out_ref, qw_ref, kv_ref, acc_ref = refs[4 + senders:]
    tokens, width_all = n_ref.shape
    head_count = width_all // HEAD_SIZE
    far_count = fq_ref.shape[0]
    col_rows = msg_refs[0].shape[0] // far_count
    for b in range(far_count):
        for s in range(senders):
            kv_ref[b, s * col_rows:(s + 1) * col_rows, :] = msg_refs[s][
                b * col_rows:(b + 1) * col_rows, :
            ]
    widen_queries(fq_ref, qw_ref, first_level)
    lane = lax.broadcasted_iota(jnp.int32, (1, LANE_BLOCK), 1)
    low_half = lane < HEAD_SIZE
    at_zero = lane == 0
    at_half = lane == HEAD_SIZE

    def block_body(j, carry):
        off = pl.multiple_of(j * LANE_BLOCK, LANE_BLOCK)
        head = j * 2
        m_blk = m_ref[:, pl.ds(off, LANE_BLOCK)]
        n_blk = n_ref[:, pl.ds(off, LANE_BLOCK)]
        d_blk = d_ref[:, pl.ds(off, LANE_BLOCK)]
        states = []
        for pick in (at_zero, at_half):
            m0 = jnp.max(jnp.where(pick, m_blk, -jnp.inf), axis=1, keepdims=True)
            d0 = jnp.sum(jnp.where(pick, d_blk, 0.0), axis=1, keepdims=True)
            states.append((m0, n_blk, d0))
        for i in range(far_count):
            level = first_level + i
            q = qw_ref[i, :, pl.ds(off, LANE_BLOCK)]
            k = kv_ref[i, :, pl.ds(off, LANE_BLOCK)]
            v = kv_ref[i, :, pl.ds(off + width_all, LANE_BLOCK)]
            gains = [gain_ref[level * head_count + head + par] for par in range(2)]
            states = level_step(states, q, k, v, gains, low_half)
        out_lo = states[0][1] / states[0][2]
        out_hi = states[1][1] / states[1][2]
        acc_ref[:, pl.ds(off, LANE_BLOCK)] = jnp.where(low_half, out_lo, out_hi).astype(
            jnp.bfloat16
        )
        return carry

    lax.fori_loop(0, width_all // LANE_BLOCK, block_body, 0)
    out_ref[...] = jnp.dot(acc_ref[...], w_ref[...], preferred_element_type=jnp.float32).astype(
        out_ref.dtype
    )


VMEM_SPEC = pl.BlockSpec(memory_space=pltpu.VMEM)
SMEM_SPEC = pl.BlockSpec(memory_space=pltpu.SMEM)


def near_attention(q0, k0, v0, near_q, near_kv, level_gain):
    tokens, width_all = q0.shape
    state = jax.ShapeDtypeStruct((tokens, width_all), jnp.float32)
    return pl.pallas_call(
        near_kernel,
        out_shape=(state, state, state),
        in_specs=[VMEM_SPEC] * 5 + [SMEM_SPEC],
        out_specs=(VMEM_SPEC, VMEM_SPEC, VMEM_SPEC),
        scratch_shapes=[pltpu.VMEM((near_q.shape[0], tokens, width_all), jnp.bfloat16)],
    )(q0, k0, v0, near_q, near_kv, level_gain)


def far_attention(first_level, m_st, n_st, d_st, far_q, messages, level_gain, weight):
    tokens, width_all = n_st.shape
    far_count = far_q.shape[0]
    return pl.pallas_call(
        functools.partial(far_kernel, first_level, len(messages)),
        out_shape=jax.ShapeDtypeStruct((tokens, width_all), jnp.bfloat16),
        in_specs=[VMEM_SPEC] * (4 + len(messages)) + [SMEM_SPEC, VMEM_SPEC],
        out_specs=VMEM_SPEC,
        scratch_shapes=[
            pltpu.VMEM((far_count, tokens, width_all), jnp.bfloat16),
            pltpu.VMEM((far_count, BLOCK, 2 * width_all), jnp.bfloat16),
            pltpu.VMEM((tokens, width_all), jnp.bfloat16),
        ],
    )(m_st, n_st, d_st, far_q, *messages, level_gain, weight)


def xor_pairs(size, bit):
    return [(i, i ^ bit) for i in range(size)]


def on_device(query_rows, key_rows, value_rows, distance_slope, out_weight):
    tokens, width_all = query_rows.shape
    head_count = distance_slope.shape[0]
    head_size = width_all // head_count
    fine_size = lax.axis_size("fine")
    coarse_size = lax.axis_size("coarse")
    local_levels = (tokens // BLOCK).bit_length() - 1
    fine_bits = fine_size.bit_length() - 1
    coarse_bits = coarse_size.bit_length() - 1
    level_total = local_levels + fine_bits + coarse_bits
    first_fine = local_levels
    first_coarse = local_levels + fine_bits
    slope_term = LOG_TWO * (1.0 - distance_slope)

    coarse_index = lax.axis_index("coarse")

    pyramid = [jnp.concatenate([query_rows, key_rows, value_rows], axis=1)]
    for _ in range(1, level_total):
        pyramid.append(coarsen(pyramid[-1]))

    def kv_of(level):
        return pyramid[level][:, width_all:]

    column = {m: kv_of(m) for m in range(first_coarse, level_total)}
    sibling_cols = []
    received_steps = []
    for bit_no in range(coarse_bits):
        level_now = first_coarse + bit_no
        pending = list(range(level_now, level_total))
        sizes = [column[m].shape[0] for m in pending]
        message = jnp.concatenate([column[m] for m in pending], axis=0)
        received = lax.ppermute(message, "coarse", xor_pairs(coarse_size, 1 << bit_no))
        received_steps.append(received)
        offsets = np.cumsum([0] + sizes)
        for i, m in enumerate(pending):
            got = received[offsets[i]:offsets[i + 1]]
            if m == level_now:
                sibling_cols.append(got)
            else:
                column[m] = jnp.concatenate([column[m], got], axis=0)

    full_weight = out_weight
    for bit_no in range(coarse_bits):
        full_weight, _ = lax.optimization_barrier(
            (full_weight, received_steps[min(bit_no + 1, coarse_bits - 1)])
        )
        got = lax.ppermute(full_weight, "coarse", xor_pairs(coarse_size, 1 << bit_no))
        upper = ((coarse_index >> bit_no) & 1) == 1
        full_weight = jnp.where(
            upper,
            jnp.concatenate([got, full_weight], axis=0),
            jnp.concatenate([full_weight, got], axis=0),
        )

    fine_keys = {l: [] for l in range(first_fine, first_coarse)}
    for offset in range(1, fine_size):
        level_now = first_fine + offset.bit_length() - 1
        fine_keys[level_now].append(
            lax.ppermute(kv_of(level_now), "fine", xor_pairs(fine_size, offset))
        )

    coarse_msg = jnp.concatenate(sibling_cols, axis=0)
    fine_msgs = [coarse_msg]
    for offset in range(1, fine_size):
        fine_msgs.append(lax.ppermute(coarse_msg, "fine", xor_pairs(fine_size, offset)))
    level_gain = jnp.concatenate([l * slope_term for l in range(level_total)])

    def padded_queries(levels):
        return jnp.stack(
            [
                jnp.pad(pyramid[l][:, :width_all], ((0, BLOCK - pyramid[l].shape[0]), (0, 0)))
                for l in levels
            ]
        )

    near_levels = list(range(first_fine, first_coarse))
    near_kv = jnp.stack([jnp.concatenate(fine_keys[l], axis=0) for l in near_levels])
    m_st, n_st, d_st = near_attention(
        query_rows, key_rows, value_rows, padded_queries(near_levels), near_kv, level_gain
    )
    return far_attention(
        first_coarse,
        m_st,
        n_st,
        d_st,
        padded_queries(list(range(first_coarse, level_total))),
        fine_msgs,
        level_gain,
        full_weight,
    )


def solution(mesh):
    return jax.shard_map(
        on_device,
        mesh=mesh,
        in_specs=(
            P(("coarse", "fine"), None),
            P(("coarse", "fine"), None),
            P(("coarse", "fine"), None),
            P(),
            P("coarse", None),
        ),
        out_specs=P(("coarse", "fine"), None),
        check_vma=False,
    )
```

```python
import functools
import math

import jax
import jax.numpy as jnp
import numpy as np
from jax import lax
from jax.experimental import pallas as pl
from jax.experimental.pallas import tpu as pltpu
from jax.sharding import PartitionSpec as P

BLOCK = 128


LOG_TWO = math.log(2.0)


def coarsen(row_data):
    dims_all = row_data.shape
    paired = row_data.reshape(dims_all[:-2] + (dims_all[-2] // 2, 2, dims_all[-1])).astype(
        jnp.float32
    )
    return ((paired[..., 0, :] + paired[..., 1, :]) * 0.5).astype(jnp.bfloat16)


HEAD_SIZE = 64
LANE_BLOCK = 128


def widen_queries(fq_ref, qw_ref, first_level):
    tokens = qw_ref.shape[1]
    rows = lax.broadcasted_iota(jnp.int32, (tokens, BLOCK), 0)
    cols = lax.broadcasted_iota(jnp.int32, (tokens, BLOCK), 1)
    for i in range(fq_ref.shape[0]):
        spread = ((rows >> (first_level + i)) == cols).astype(jnp.bfloat16)
        qw_ref[i] = jnp.dot(spread, fq_ref[i], preferred_element_type=jnp.float32).astype(
            jnp.bfloat16
        )


def level_step(states, q, k, v, gains, low_half):
    scale = 1.0 / math.sqrt(HEAD_SIZE)
    new_states = []
    for par, gain in enumerate(gains):
        keep = low_half if par == 0 else jnp.logical_not(low_half)
        qm = jnp.where(keep, q, jnp.zeros_like(q))
        s = lax.dot_general(qm, k, (((1,), (1,)), ((), ())), preferred_element_type=jnp.float32)
        s = s * scale + gain
        m = jnp.max(s, axis=1, keepdims=True)
        p = jnp.exp(s - m).astype(jnp.bfloat16)
        d = jnp.sum(p.astype(jnp.float32), axis=1, keepdims=True)
        n = jnp.dot(p, v, preferred_element_type=jnp.float32)
        if states is None:
            new_states.append((m, n, d))
        else:
            ma, na, da = states[par]
            mx = jnp.maximum(ma, m)
            sa = jnp.exp(ma - mx)
            sb = jnp.exp(m - mx)
            new_states.append((mx, na * sa + n * sb, da * sa + d * sb))
    return new_states


def near_kernel(q0_ref, k0_ref, v0_ref, fq_ref, fkv_ref, gain_ref, m_ref, n_ref, d_ref, qw_ref):
    tokens, width_all = q0_ref.shape
    head_count = width_all // HEAD_SIZE
    widen_queries(fq_ref, qw_ref, 1)
    lane = lax.broadcasted_iota(jnp.int32, (1, LANE_BLOCK), 1)
    low_half = lane < HEAD_SIZE

    def block_body(j, carry):
        off = pl.multiple_of(j * LANE_BLOCK, LANE_BLOCK)
        head = j * 2
        states = None
        for level in range(fq_ref.shape[0] + 1):
            if level == 0:
                q = q0_ref[:, pl.ds(off, LANE_BLOCK)]
                k = k0_ref[:, pl.ds(off, LANE_BLOCK)]
                v = v0_ref[:, pl.ds(off, LANE_BLOCK)]
            else:
                q = qw_ref[level - 1, :, pl.ds(off, LANE_BLOCK)]
                k = fkv_ref[level - 1, :, pl.ds(off, LANE_BLOCK)]
                v = fkv_ref[level - 1, :, pl.ds(off + width_all, LANE_BLOCK)]
            gains = [gain_ref[level * head_count + head + par] for par in range(2)]
            states = level_step(states, q, k, v, gains, low_half)
        shape = (tokens, LANE_BLOCK)
        m_ref[:, pl.ds(off, LANE_BLOCK)] = jnp.where(
            low_half, jnp.broadcast_to(states[0][0], shape), jnp.broadcast_to(states[1][0], shape)
        )
        n_ref[:, pl.ds(off, LANE_BLOCK)] = jnp.where(low_half, states[0][1], states[1][1])
        d_ref[:, pl.ds(off, LANE_BLOCK)] = jnp.where(
            low_half, jnp.broadcast_to(states[0][2], shape), jnp.broadcast_to(states[1][2], shape)
        )
        return carry

    lax.fori_loop(0, width_all // LANE_BLOCK, block_body, 0)


def far_kernel(first_level, senders, *refs):
    m_ref, n_ref, d_ref, fq_ref = refs[:4]
    msg_refs = refs[4:4 + senders]
    gain_ref, out_ref, qw_ref, kv_ref = refs[4 + senders:]
    tokens, width_all = n_ref.shape
    head_count = width_all // HEAD_SIZE
    far_count = fq_ref.shape[0]
    col_rows = msg_refs[0].shape[0] // far_count
    for b in range(far_count):
        for s in range(senders):
            kv_ref[b, s * col_rows:(s + 1) * col_rows, :] = msg_refs[s][
                b * col_rows:(b + 1) * col_rows, :
            ]
    widen_queries(fq_ref, qw_ref, first_level)
    lane = lax.broadcasted_iota(jnp.int32, (1, LANE_BLOCK), 1)
    low_half = lane < HEAD_SIZE
    at_zero = lane == 0
    at_half = lane == HEAD_SIZE

    def block_body(j, carry):
        off = pl.multiple_of(j * LANE_BLOCK, LANE_BLOCK)
        head = j * 2
        m_blk = m_ref[:, pl.ds(off, LANE_BLOCK)]
        n_blk = n_ref[:, pl.ds(off, LANE_BLOCK)]
        d_blk = d_ref[:, pl.ds(off, LANE_BLOCK)]
        states = []
        for pick in (at_zero, at_half):
            m0 = jnp.max(jnp.where(pick, m_blk, -jnp.inf), axis=1, keepdims=True)
            d0 = jnp.sum(jnp.where(pick, d_blk, 0.0), axis=1, keepdims=True)
            states.append((m0, n_blk, d0))
        for i in range(far_count):
            level = first_level + i
            q = qw_ref[i, :, pl.ds(off, LANE_BLOCK)]
            k = kv_ref[i, :, pl.ds(off, LANE_BLOCK)]
            v = kv_ref[i, :, pl.ds(off + width_all, LANE_BLOCK)]
            gains = [gain_ref[level * head_count + head + par] for par in range(2)]
            states = level_step(states, q, k, v, gains, low_half)
        out_lo = states[0][1] / states[0][2]
        out_hi = states[1][1] / states[1][2]
        out_ref[:, pl.ds(off, LANE_BLOCK)] = jnp.where(low_half, out_lo, out_hi).astype(
            out_ref.dtype
        )
        return carry

    lax.fori_loop(0, width_all // LANE_BLOCK, block_body, 0)


VMEM_SPEC = pl.BlockSpec(memory_space=pltpu.VMEM)
SMEM_SPEC = pl.BlockSpec(memory_space=pltpu.SMEM)


def near_attention(q0, k0, v0, near_q, near_kv, level_gain):
    tokens, width_all = q0.shape
    state = jax.ShapeDtypeStruct((tokens, width_all), jnp.float32)
    return pl.pallas_call(
        near_kernel,
        out_shape=(state, state, state),
        in_specs=[VMEM_SPEC] * 5 + [SMEM_SPEC],
        out_specs=(VMEM_SPEC, VMEM_SPEC, VMEM_SPEC),
        scratch_shapes=[pltpu.VMEM((near_q.shape[0], tokens, width_all), jnp.bfloat16)],
    )(q0, k0, v0, near_q, near_kv, level_gain)


def far_attention(first_level, m_st, n_st, d_st, far_q, messages, level_gain):
    tokens, width_all = n_st.shape
    far_count = far_q.shape[0]
    return pl.pallas_call(
        functools.partial(far_kernel, first_level, len(messages)),
        out_shape=jax.ShapeDtypeStruct((tokens, width_all), jnp.bfloat16),
        in_specs=[VMEM_SPEC] * (4 + len(messages)) + [SMEM_SPEC],
        out_specs=VMEM_SPEC,
        scratch_shapes=[
            pltpu.VMEM((far_count, tokens, width_all), jnp.bfloat16),
            pltpu.VMEM((far_count, BLOCK, 2 * width_all), jnp.bfloat16),
        ],
    )(m_st, n_st, d_st, far_q, *messages, level_gain)


def xor_pairs(size, bit):
    return [(i, i ^ bit) for i in range(size)]


def on_device(query_rows, key_rows, value_rows, distance_slope, out_weight):
    tokens, width_all = query_rows.shape
    head_count = distance_slope.shape[0]
    head_size = width_all // head_count
    fine_size = lax.axis_size("fine")
    coarse_size = lax.axis_size("coarse")
    local_levels = (tokens // BLOCK).bit_length() - 1
    fine_bits = fine_size.bit_length() - 1
    coarse_bits = coarse_size.bit_length() - 1
    level_total = local_levels + fine_bits + coarse_bits
    first_fine = local_levels
    first_coarse = local_levels + fine_bits
    slope_term = LOG_TWO * (1.0 - distance_slope)

    full_weight = lax.all_gather(out_weight, "coarse", axis=0, tiled=True)

    pyramid = [jnp.concatenate([query_rows, key_rows, value_rows], axis=1)]
    for _ in range(1, level_total):
        pyramid.append(coarsen(pyramid[-1]))

    def kv_of(level):
        return pyramid[level][:, width_all:]

    column = {m: kv_of(m) for m in range(first_coarse, level_total)}
    sibling_cols = []
    for bit_no in range(coarse_bits):
        level_now = first_coarse + bit_no
        pending = list(range(level_now, level_total))
        sizes = [column[m].shape[0] for m in pending]
        message = jnp.concatenate([column[m] for m in pending], axis=0)
        received = lax.ppermute(message, "coarse", xor_pairs(coarse_size, 1 << bit_no))
        offsets = np.cumsum([0] + sizes)
        for i, m in enumerate(pending):
            got = received[offsets[i]:offsets[i + 1]]
            if m == level_now:
                sibling_cols.append(got)
            else:
                column[m] = jnp.concatenate([column[m], got], axis=0)

    fine_keys = {l: [] for l in range(first_fine, first_coarse)}
    for offset in range(1, fine_size):
        level_now = first_fine + offset.bit_length() - 1
        fine_keys[level_now].append(
            lax.ppermute(kv_of(level_now), "fine", xor_pairs(fine_size, offset))
        )

    coarse_msg = jnp.concatenate(sibling_cols, axis=0)
    fine_msgs = [coarse_msg]
    for offset in range(1, fine_size):
        fine_msgs.append(lax.ppermute(coarse_msg, "fine", xor_pairs(fine_size, offset)))
    level_gain = jnp.concatenate([l * slope_term for l in range(level_total)])

    def padded_queries(levels):
        return jnp.stack(
            [
                jnp.pad(pyramid[l][:, :width_all], ((0, BLOCK - pyramid[l].shape[0]), (0, 0)))
                for l in levels
            ]
        )

    near_levels = list(range(first_fine, first_coarse))
    near_kv = jnp.stack([jnp.concatenate(fine_keys[l], axis=0) for l in near_levels])
    m_st, n_st, d_st = near_attention(
        query_rows, key_rows, value_rows, padded_queries(near_levels), near_kv, level_gain
    )
    attended = far_attention(
        first_coarse,
        m_st,
        n_st,
        d_st,
        padded_queries(list(range(first_coarse, level_total))),
        fine_msgs,
        level_gain,
    )
    projected = jnp.dot(attended, full_weight, preferred_element_type=jnp.float32)
    return projected.astype(jnp.bfloat16)


def solution(mesh):
    return jax.shard_map(
        on_device,
        mesh=mesh,
        in_specs=(
            P(("coarse", "fine"), None),
            P(("coarse", "fine"), None),
            P(("coarse", "fine"), None),
            P(),
            P("coarse", None),
        ),
        out_specs=P(("coarse", "fine"), None),
        check_vma=False,
    )
```

```python
import functools
import math

import jax
import jax.numpy as jnp
import numpy as np
from jax import lax
from jax.experimental import pallas as pl
from jax.experimental.pallas import tpu as pltpu
from jax.sharding import PartitionSpec as P

BLOCK = 128


LOG_TWO = math.log(2.0)


def coarsen(row_data):
    dims_all = row_data.shape
    paired = row_data.reshape(dims_all[:-2] + (dims_all[-2] // 2, 2, dims_all[-1])).astype(
        jnp.float32
    )
    return ((paired[..., 0, :] + paired[..., 1, :]) * 0.5).astype(jnp.bfloat16)


HEAD_SIZE = 64
LANE_BLOCK = 128


def widen_queries(fq_ref, qw_ref, first_level):
    tokens = qw_ref.shape[1]
    rows = lax.broadcasted_iota(jnp.int32, (tokens, BLOCK), 0)
    cols = lax.broadcasted_iota(jnp.int32, (tokens, BLOCK), 1)
    for i in range(fq_ref.shape[0]):
        spread = ((rows >> (first_level + i)) == cols).astype(jnp.bfloat16)
        qw_ref[i] = jnp.dot(spread, fq_ref[i], preferred_element_type=jnp.float32).astype(
            jnp.bfloat16
        )


def level_step(states, q, k, v, gains, low_half):
    scale = 1.0 / math.sqrt(HEAD_SIZE)
    new_states = []
    for par, gain in enumerate(gains):
        keep = low_half if par == 0 else jnp.logical_not(low_half)
        qm = jnp.where(keep, q, jnp.zeros_like(q))
        s = lax.dot_general(qm, k, (((1,), (1,)), ((), ())), preferred_element_type=jnp.float32)
        s = s * scale + gain
        m = jnp.max(s, axis=1, keepdims=True)
        p = jnp.exp(s - m).astype(jnp.bfloat16)
        d = jnp.sum(p.astype(jnp.float32), axis=1, keepdims=True)
        n = jnp.dot(p, v, preferred_element_type=jnp.float32)
        if states is None:
            new_states.append((m, n, d))
        else:
            ma, na, da = states[par]
            mx = jnp.maximum(ma, m)
            sa = jnp.exp(ma - mx)
            sb = jnp.exp(m - mx)
            new_states.append((mx, na * sa + n * sb, da * sa + d * sb))
    return new_states


def near_kernel(q0_ref, k0_ref, v0_ref, fq_ref, fkv_ref, gain_ref, m_ref, n_ref, d_ref, qw_ref):
    tokens, width_all = q0_ref.shape
    head_count = width_all // HEAD_SIZE
    widen_queries(fq_ref, qw_ref, 1)
    lane = lax.broadcasted_iota(jnp.int32, (1, LANE_BLOCK), 1)
    low_half = lane < HEAD_SIZE

    def block_body(j, carry):
        off = pl.multiple_of(j * LANE_BLOCK, LANE_BLOCK)
        head = j * 2
        states = None
        for level in range(fq_ref.shape[0] + 1):
            if level == 0:
                q = q0_ref[:, pl.ds(off, LANE_BLOCK)]
                k = k0_ref[:, pl.ds(off, LANE_BLOCK)]
                v = v0_ref[:, pl.ds(off, LANE_BLOCK)]
            else:
                q = qw_ref[level - 1, :, pl.ds(off, LANE_BLOCK)]
                k = fkv_ref[level - 1, :, pl.ds(off, LANE_BLOCK)]
                v = fkv_ref[level - 1, :, pl.ds(off + width_all, LANE_BLOCK)]
            gains = [gain_ref[level * head_count + head + par] for par in range(2)]
            states = level_step(states, q, k, v, gains, low_half)
        shape = (tokens, LANE_BLOCK)
        m_ref[:, pl.ds(off, LANE_BLOCK)] = jnp.where(
            low_half, jnp.broadcast_to(states[0][0], shape), jnp.broadcast_to(states[1][0], shape)
        )
        n_ref[:, pl.ds(off, LANE_BLOCK)] = jnp.where(low_half, states[0][1], states[1][1])
        d_ref[:, pl.ds(off, LANE_BLOCK)] = jnp.where(
            low_half, jnp.broadcast_to(states[0][2], shape), jnp.broadcast_to(states[1][2], shape)
        )
        return carry

    lax.fori_loop(0, width_all // LANE_BLOCK, block_body, 0)


def far_kernel(first_level, senders, *refs):
    m_ref, n_ref, d_ref, fq_ref = refs[:4]
    msg_refs = refs[4:4 + senders]
    gain_ref, out_ref, qw_ref, kv_ref = refs[4 + senders:]
    tokens, width_all = n_ref.shape
    head_count = width_all // HEAD_SIZE
    far_count = fq_ref.shape[0]
    col_rows = msg_refs[0].shape[0] // far_count
    for b in range(far_count):
        for s in range(senders):
            kv_ref[b, s * col_rows:(s + 1) * col_rows, :] = msg_refs[s][
                b * col_rows:(b + 1) * col_rows, :
            ]
    widen_queries(fq_ref, qw_ref, first_level)
    lane = lax.broadcasted_iota(jnp.int32, (1, LANE_BLOCK), 1)
    low_half = lane < HEAD_SIZE
    at_zero = lane == 0
    at_half = lane == HEAD_SIZE

    def block_body(j, carry):
        off = pl.multiple_of(j * LANE_BLOCK, LANE_BLOCK)
        head = j * 2
        m_blk = m_ref[:, pl.ds(off, LANE_BLOCK)]
        n_blk = n_ref[:, pl.ds(off, LANE_BLOCK)]
        d_blk = d_ref[:, pl.ds(off, LANE_BLOCK)]
        states = []
        for pick in (at_zero, at_half):
            m0 = jnp.max(jnp.where(pick, m_blk, -jnp.inf), axis=1, keepdims=True)
            d0 = jnp.sum(jnp.where(pick, d_blk, 0.0), axis=1, keepdims=True)
            states.append((m0, n_blk, d0))
        for i in range(far_count):
            level = first_level + i
            q = qw_ref[i, :, pl.ds(off, LANE_BLOCK)]
            k = kv_ref[i, :, pl.ds(off, LANE_BLOCK)]
            v = kv_ref[i, :, pl.ds(off + width_all, LANE_BLOCK)]
            gains = [gain_ref[level * head_count + head + par] for par in range(2)]
            states = level_step(states, q, k, v, gains, low_half)
        out_lo = states[0][1] / states[0][2]
        out_hi = states[1][1] / states[1][2]
        out_ref[:, pl.ds(off, LANE_BLOCK)] = jnp.where(low_half, out_lo, out_hi).astype(
            out_ref.dtype
        )
        return carry

    lax.fori_loop(0, width_all // LANE_BLOCK, block_body, 0)


VMEM_SPEC = pl.BlockSpec(memory_space=pltpu.VMEM)
SMEM_SPEC = pl.BlockSpec(memory_space=pltpu.SMEM)


def near_attention(q0, k0, v0, near_q, near_kv, level_gain):
    tokens, width_all = q0.shape
    state = jax.ShapeDtypeStruct((tokens, width_all), jnp.float32)
    return pl.pallas_call(
        near_kernel,
        out_shape=(state, state, state),
        in_specs=[VMEM_SPEC] * 5 + [SMEM_SPEC],
        out_specs=(VMEM_SPEC, VMEM_SPEC, VMEM_SPEC),
        scratch_shapes=[pltpu.VMEM((near_q.shape[0], tokens, width_all), jnp.bfloat16)],
    )(q0, k0, v0, near_q, near_kv, level_gain)


def far_attention(first_level, m_st, n_st, d_st, far_q, messages, level_gain):
    tokens, width_all = n_st.shape
    far_count = far_q.shape[0]
    return pl.pallas_call(
        functools.partial(far_kernel, first_level, len(messages)),
        out_shape=jax.ShapeDtypeStruct((tokens, width_all), jnp.bfloat16),
        in_specs=[VMEM_SPEC] * (4 + len(messages)) + [SMEM_SPEC],
        out_specs=VMEM_SPEC,
        scratch_shapes=[
            pltpu.VMEM((far_count, tokens, width_all), jnp.bfloat16),
            pltpu.VMEM((far_count, BLOCK, 2 * width_all), jnp.bfloat16),
        ],
    )(m_st, n_st, d_st, far_q, *messages, level_gain)


def xor_pairs(size, bit):
    return [(i, i ^ bit) for i in range(size)]


def on_device(query_rows, key_rows, value_rows, distance_slope, out_weight):
    tokens, width_all = query_rows.shape
    head_count = distance_slope.shape[0]
    head_size = width_all // head_count
    fine_size = lax.axis_size("fine")
    coarse_size = lax.axis_size("coarse")
    local_levels = (tokens // BLOCK).bit_length() - 1
    fine_bits = fine_size.bit_length() - 1
    coarse_bits = coarse_size.bit_length() - 1
    level_total = local_levels + fine_bits + coarse_bits
    first_fine = local_levels
    first_coarse = local_levels + fine_bits
    slope_term = LOG_TWO * (1.0 - distance_slope)

    full_weight = lax.all_gather(out_weight, "coarse", axis=0, tiled=True)

    kv_pyramid = [jnp.concatenate([key_rows, value_rows], axis=1)]
    q_pyramid = [query_rows]
    for _ in range(1, level_total):
        kv_pyramid.append(coarsen(kv_pyramid[-1]))
        q_pyramid.append(coarsen(q_pyramid[-1]))

    def kv_of(level):
        return kv_pyramid[level]

    column = {m: kv_of(m) for m in range(first_coarse, level_total)}
    sibling_cols = []
    for bit_no in range(coarse_bits):
        level_now = first_coarse + bit_no
        pending = list(range(level_now, level_total))
        sizes = [column[m].shape[0] for m in pending]
        message = jnp.concatenate([column[m] for m in pending], axis=0)
        received = lax.ppermute(message, "coarse", xor_pairs(coarse_size, 1 << bit_no))
        offsets = np.cumsum([0] + sizes)
        for i, m in enumerate(pending):
            got = received[offsets[i]:offsets[i + 1]]
            if m == level_now:
                sibling_cols.append(got)
            else:
                column[m] = jnp.concatenate([column[m], got], axis=0)

    fine_keys = {l: [] for l in range(first_fine, first_coarse)}
    for offset in range(1, fine_size):
        level_now = first_fine + offset.bit_length() - 1
        fine_keys[level_now].append(
            lax.ppermute(kv_of(level_now), "fine", xor_pairs(fine_size, offset))
        )

    coarse_msg = jnp.concatenate(sibling_cols, axis=0)
    fine_msgs = [coarse_msg]
    for offset in range(1, fine_size):
        fine_msgs.append(lax.ppermute(coarse_msg, "fine", xor_pairs(fine_size, offset)))
    level_gain = jnp.concatenate([l * slope_term for l in range(level_total)])

    def padded_queries(levels):
        return jnp.stack(
            [
                jnp.pad(q_pyramid[l], ((0, BLOCK - q_pyramid[l].shape[0]), (0, 0)))
                for l in levels
            ]
        )

    near_levels = list(range(first_fine, first_coarse))
    near_kv = jnp.stack([jnp.concatenate(fine_keys[l], axis=0) for l in near_levels])
    m_st, n_st, d_st = near_attention(
        query_rows, key_rows, value_rows, padded_queries(near_levels), near_kv, level_gain
    )
    attended = far_attention(
        first_coarse,
        m_st,
        n_st,
        d_st,
        padded_queries(list(range(first_coarse, level_total))),
        fine_msgs,
        level_gain,
    )
    projected = jnp.dot(attended, full_weight, preferred_element_type=jnp.float32)
    return projected.astype(jnp.bfloat16)


def solution(mesh):
    return jax.shard_map(
        on_device,
        mesh=mesh,
        in_specs=(
            P(("coarse", "fine"), None),
            P(("coarse", "fine"), None),
            P(("coarse", "fine"), None),
            P(),
            P("coarse", None),
        ),
        out_specs=P(("coarse", "fine"), None),
        check_vma=False,
    )
```

```python
import functools
import math

import jax
import jax.numpy as jnp
import numpy as np
from jax import lax
from jax.experimental import pallas as pl
from jax.experimental.pallas import tpu as pltpu
from jax.sharding import PartitionSpec as P

BLOCK = 128


LOG_TWO = math.log(2.0)


def coarsen(row_data):
    dims_all = row_data.shape
    paired = row_data.reshape(dims_all[:-2] + (dims_all[-2] // 2, 2, dims_all[-1])).astype(
        jnp.float32
    )
    return ((paired[..., 0, :] + paired[..., 1, :]) * 0.5).astype(jnp.bfloat16)


HEAD_SIZE = 64
LANE_BLOCK = 128


def widen_queries(fq_ref, qw_ref, first_level):
    tokens = qw_ref.shape[1]
    rows = lax.broadcasted_iota(jnp.int32, (tokens, BLOCK), 0)
    cols = lax.broadcasted_iota(jnp.int32, (tokens, BLOCK), 1)
    for i in range(fq_ref.shape[0]):
        spread = ((rows >> (first_level + i)) == cols).astype(jnp.bfloat16)
        qw_ref[i] = jnp.dot(spread, fq_ref[i], preferred_element_type=jnp.float32).astype(
            jnp.bfloat16
        )


def level_step(states, q, k, v, gains, low_half):
    scale = 1.0 / math.sqrt(HEAD_SIZE)
    new_states = []
    for par, gain in enumerate(gains):
        keep = low_half if par == 0 else jnp.logical_not(low_half)
        qm = jnp.where(keep, q, jnp.zeros_like(q))
        s = lax.dot_general(qm, k, (((1,), (1,)), ((), ())), preferred_element_type=jnp.float32)
        s = s * scale + gain
        m = jnp.max(s, axis=1, keepdims=True)
        p = jnp.exp(s - m).astype(jnp.bfloat16)
        d = jnp.sum(p.astype(jnp.float32), axis=1, keepdims=True)
        n = jnp.dot(p, v, preferred_element_type=jnp.float32)
        if states is None:
            new_states.append((m, n, d))
        else:
            ma, na, da = states[par]
            mx = jnp.maximum(ma, m)
            sa = jnp.exp(ma - mx)
            sb = jnp.exp(m - mx)
            new_states.append((mx, na * sa + n * sb, da * sa + d * sb))
    return new_states


def near_kernel(
    far_level, q0_ref, k0_ref, v0_ref, fq_ref, fkv_ref, ffq_ref, gain_ref, m_ref, n_ref, d_ref,
    fqw_ref, qw_ref,
):
    tokens, width_all = q0_ref.shape
    head_count = width_all // HEAD_SIZE
    widen_queries(fq_ref, qw_ref, 1)
    widen_queries(ffq_ref, fqw_ref, far_level)
    lane = lax.broadcasted_iota(jnp.int32, (1, LANE_BLOCK), 1)
    low_half = lane < HEAD_SIZE

    def block_body(j, carry):
        off = pl.multiple_of(j * LANE_BLOCK, LANE_BLOCK)
        head = j * 2
        states = None
        for level in range(fq_ref.shape[0] + 1):
            if level == 0:
                q = q0_ref[:, pl.ds(off, LANE_BLOCK)]
                k = k0_ref[:, pl.ds(off, LANE_BLOCK)]
                v = v0_ref[:, pl.ds(off, LANE_BLOCK)]
            else:
                q = qw_ref[level - 1, :, pl.ds(off, LANE_BLOCK)]
                k = fkv_ref[level - 1, :, pl.ds(off, LANE_BLOCK)]
                v = fkv_ref[level - 1, :, pl.ds(off + width_all, LANE_BLOCK)]
            gains = [gain_ref[level * head_count + head + par] for par in range(2)]
            states = level_step(states, q, k, v, gains, low_half)
        shape = (tokens, LANE_BLOCK)
        m_ref[:, pl.ds(off, LANE_BLOCK)] = jnp.where(
            low_half, jnp.broadcast_to(states[0][0], shape), jnp.broadcast_to(states[1][0], shape)
        )
        n_ref[:, pl.ds(off, LANE_BLOCK)] = jnp.where(low_half, states[0][1], states[1][1])
        d_ref[:, pl.ds(off, LANE_BLOCK)] = jnp.where(
            low_half, jnp.broadcast_to(states[0][2], shape), jnp.broadcast_to(states[1][2], shape)
        )
        return carry

    lax.fori_loop(0, width_all // LANE_BLOCK, block_body, 0)


def far_kernel(first_level, senders, *refs):
    m_ref, n_ref, d_ref, qw_ref = refs[:4]
    msg_refs = refs[4:4 + senders]
    gain_ref, out_ref, kv_ref = refs[4 + senders:]
    tokens, width_all = n_ref.shape
    head_count = width_all // HEAD_SIZE
    far_count = qw_ref.shape[0]
    col_rows = msg_refs[0].shape[0] // far_count
    for b in range(far_count):
        for s in range(senders):
            kv_ref[b, s * col_rows:(s + 1) * col_rows, :] = msg_refs[s][
                b * col_rows:(b + 1) * col_rows, :
            ]
    lane = lax.broadcasted_iota(jnp.int32, (1, LANE_BLOCK), 1)
    low_half = lane < HEAD_SIZE
    at_zero = lane == 0
    at_half = lane == HEAD_SIZE

    def block_body(j, carry):
        off = pl.multiple_of(j * LANE_BLOCK, LANE_BLOCK)
        head = j * 2
        m_blk = m_ref[:, pl.ds(off, LANE_BLOCK)]
        n_blk = n_ref[:, pl.ds(off, LANE_BLOCK)]
        d_blk = d_ref[:, pl.ds(off, LANE_BLOCK)]
        states = []
        for pick in (at_zero, at_half):
            m0 = jnp.max(jnp.where(pick, m_blk, -jnp.inf), axis=1, keepdims=True)
            d0 = jnp.sum(jnp.where(pick, d_blk, 0.0), axis=1, keepdims=True)
            states.append((m0, n_blk, d0))
        for i in range(far_count):
            level = first_level + i
            q = qw_ref[i, :, pl.ds(off, LANE_BLOCK)]
            k = kv_ref[i, :, pl.ds(off, LANE_BLOCK)]
            v = kv_ref[i, :, pl.ds(off + width_all, LANE_BLOCK)]
            gains = [gain_ref[level * head_count + head + par] for par in range(2)]
            states = level_step(states, q, k, v, gains, low_half)
        out_lo = states[0][1] / states[0][2]
        out_hi = states[1][1] / states[1][2]
        out_ref[:, pl.ds(off, LANE_BLOCK)] = jnp.where(low_half, out_lo, out_hi).astype(
            out_ref.dtype
        )
        return carry

    lax.fori_loop(0, width_all // LANE_BLOCK, block_body, 0)


VMEM_SPEC = pl.BlockSpec(memory_space=pltpu.VMEM)
SMEM_SPEC = pl.BlockSpec(memory_space=pltpu.SMEM)


def near_attention(far_level, q0, k0, v0, near_q, near_kv, far_q, level_gain):
    tokens, width_all = q0.shape
    state = jax.ShapeDtypeStruct((tokens, width_all), jnp.float32)
    widened = jax.ShapeDtypeStruct((far_q.shape[0], tokens, width_all), jnp.bfloat16)
    return pl.pallas_call(
        functools.partial(near_kernel, far_level),
        out_shape=(state, state, state, widened),
        in_specs=[VMEM_SPEC] * 6 + [SMEM_SPEC],
        out_specs=(VMEM_SPEC, VMEM_SPEC, VMEM_SPEC, VMEM_SPEC),
        scratch_shapes=[pltpu.VMEM((near_q.shape[0], tokens, width_all), jnp.bfloat16)],
    )(q0, k0, v0, near_q, near_kv, far_q, level_gain)


def far_attention(first_level, m_st, n_st, d_st, far_q, messages, level_gain):
    tokens, width_all = n_st.shape
    far_count = far_q.shape[0]
    return pl.pallas_call(
        functools.partial(far_kernel, first_level, len(messages)),
        out_shape=jax.ShapeDtypeStruct((tokens, width_all), jnp.bfloat16),
        in_specs=[VMEM_SPEC] * (4 + len(messages)) + [SMEM_SPEC],
        out_specs=VMEM_SPEC,
        scratch_shapes=[pltpu.VMEM((far_count, BLOCK, 2 * width_all), jnp.bfloat16)],
    )(m_st, n_st, d_st, far_q, *messages, level_gain)


def xor_pairs(size, bit):
    return [(i, i ^ bit) for i in range(size)]


def on_device(query_rows, key_rows, value_rows, distance_slope, out_weight):
    tokens, width_all = query_rows.shape
    head_count = distance_slope.shape[0]
    head_size = width_all // head_count
    fine_size = lax.axis_size("fine")
    coarse_size = lax.axis_size("coarse")
    local_levels = (tokens // BLOCK).bit_length() - 1
    fine_bits = fine_size.bit_length() - 1
    coarse_bits = coarse_size.bit_length() - 1
    level_total = local_levels + fine_bits + coarse_bits
    first_fine = local_levels
    first_coarse = local_levels + fine_bits
    slope_term = LOG_TWO * (1.0 - distance_slope)

    full_weight = lax.all_gather(out_weight, "coarse", axis=0, tiled=True)

    kv_pyramid = [jnp.concatenate([key_rows, value_rows], axis=1)]
    q_pyramid = [query_rows]
    for _ in range(1, level_total):
        kv_pyramid.append(coarsen(kv_pyramid[-1]))
        q_pyramid.append(coarsen(q_pyramid[-1]))

    def kv_of(level):
        return kv_pyramid[level]

    column = {m: kv_of(m) for m in range(first_coarse, level_total)}
    sibling_cols = []
    for bit_no in range(coarse_bits):
        level_now = first_coarse + bit_no
        pending = list(range(level_now, level_total))
        sizes = [column[m].shape[0] for m in pending]
        message = jnp.concatenate([column[m] for m in pending], axis=0)
        received = lax.ppermute(message, "coarse", xor_pairs(coarse_size, 1 << bit_no))
        offsets = np.cumsum([0] + sizes)
        for i, m in enumerate(pending):
            got = received[offsets[i]:offsets[i + 1]]
            if m == level_now:
                sibling_cols.append(got)
            else:
                column[m] = jnp.concatenate([column[m], got], axis=0)

    fine_keys = {l: [] for l in range(first_fine, first_coarse)}
    for offset in range(1, fine_size):
        level_now = first_fine + offset.bit_length() - 1
        fine_keys[level_now].append(
            lax.ppermute(kv_of(level_now), "fine", xor_pairs(fine_size, offset))
        )

    coarse_msg = jnp.concatenate(sibling_cols, axis=0)
    fine_msgs = [coarse_msg]
    for offset in range(1, fine_size):
        fine_msgs.append(lax.ppermute(coarse_msg, "fine", xor_pairs(fine_size, offset)))
    level_gain = jnp.concatenate([l * slope_term for l in range(level_total)])

    def padded_queries(levels):
        return jnp.stack(
            [
                jnp.pad(q_pyramid[l], ((0, BLOCK - q_pyramid[l].shape[0]), (0, 0)))
                for l in levels
            ]
        )

    near_levels = list(range(first_fine, first_coarse))
    near_kv = jnp.stack([jnp.concatenate(fine_keys[l], axis=0) for l in near_levels])
    m_st, n_st, d_st, far_wide = near_attention(
        first_coarse,
        query_rows,
        key_rows,
        value_rows,
        padded_queries(near_levels),
        near_kv,
        padded_queries(list(range(first_coarse, level_total))),
        level_gain,
    )
    attended = far_attention(
        first_coarse,
        m_st,
        n_st,
        d_st,
        far_wide,
        fine_msgs,
        level_gain,
    )
    projected = jnp.dot(attended, full_weight, preferred_element_type=jnp.float32)
    return projected.astype(jnp.bfloat16)


def solution(mesh):
    return jax.shard_map(
        on_device,
        mesh=mesh,
        in_specs=(
            P(("coarse", "fine"), None),
            P(("coarse", "fine"), None),
            P(("coarse", "fine"), None),
            P(),
            P("coarse", None),
        ),
        out_specs=P(("coarse", "fine"), None),
        check_vma=False,
    )
```
